32 devices in a mesh: grp: 2 (over y), ctx: 4 (over z), chan: 2 (over x), dec: 2 (over core).
Axes of the slice: x: 2, y: 2, z: 4, core: 2. Of those that a mesh axis runs over, the one named last changes fastest.
Arguments:
- projected: bfloat16 [3, 2048, 8192], P(None, ('grp', 'ctx', 'dec'), 'chan'), parts along dimension 1, may hold values from -6 to 6
- short_filters: float32 [3, 3, 8192], P(None, None, 'chan'), may hold values from -3 to 3
- decay_rate: float32 [16, 8192], P(None, 'chan'), may hold values from 9.765625e-05 to 0.1, as said below
- residue: float32 [16, 8192], P(None, 'chan'), may hold values from -1 to 1
- skip: float32 [8192], P('chan'), may hold values from -4 to 4
Outputs:
- mixed: bfloat16 [2048, 8192], P(('grp', 'ctx', 'dec'), 'chan'), parts along dimension 0
- final_state: float32 [32, 8192], P('grp', 'chan'), parts along dimension 0
The draws below stay inside these ranges and needn't reach their ends.
There are 2 independent parts, one for each index of `grp`. The reference program is written for one: setup_inputs(seed, part) draws one part's arguments, and reference() takes and returns one part's arrays. A program takes and returns all parts, laid end to end along the dimension named above; an argument that names none is the same for every part. Nothing has to cross between parts.
Inputs may be any that keep to these rules, and one draw needn't show every extreme that they name: `decay_rate`: positive.
All inputs are finite; a program needn't handle non-finite values.
Results may differ from the reference program's by a relative error of at most 0.001.
Values may be sent and summed in bfloat16 or wider, within the bound.
No kernel may reach another device: no remote copies, remote signals or barrier semaphores. Data moves between devices by JAX's collectives and lax.ppermute only.
A program may use at most 256 MiB of HBM per device.

```python
import math
import jax
import jax.numpy as jnp
from jax import lax

D = 8192
MODES = 16
TAPS = 3
TOK_DEV = 128
TOKENS = 1024


def rate_table(key):
    chooser = jax.random.uniform(jax.random.fold_in(key, 11), (MODES, D), jnp.float32)
    position_u = jax.random.uniform(jax.random.fold_in(key, 12), (MODES, D), jnp.float32)
    slow_share = 0.35
    middle_share = 0.35
    slow_rate = 0.1 / TOKENS * jnp.exp(position_u * math.log(20.0))
    middle_rate = 0.06 / TOK_DEV * jnp.exp(position_u * math.log(2.0 / 0.06))
    fast_rate = 1.0 / 60.0 * jnp.exp(position_u * math.log(6.0))
    upper = jnp.where(chooser < slow_share + middle_share, middle_rate, fast_rate)
    return jnp.where(chooser < slow_share, slow_rate, upper)


def draw_decay_rate(key, part):
    return rate_table(key)


def draw_residue(key, part):
    rates = rate_table(key)
    normal_part = jax.random.truncated_normal(jax.random.fold_in(key, 13), -4.0, 4.0, (MODES, D), jnp.float32)
    return normal_part * jnp.sqrt(2.0 * (rates + 1.0 / TOKENS) / MODES)


def steps_of(stream_key, extent, shards, smallest, top_value):
    def one(position, blocks):
        steps = jax.random.uniform(jax.random.fold_in(jax.random.fold_in(stream_key, 6), position), (blocks,), jnp.float32, smallest / len(shards), top_value / len(shards))
        return jnp.repeat(jnp.exp(steps), extent[position] // blocks).reshape((-1,) + (1,) * (len(extent) - position - 1))

    loudness = one(*shards[0])
    for cut in shards[1:]:
        loudness = loudness * one(*cut)
    return loudness


def gaussian(key, extent, scale, bound, pieces=(), held_as=jnp.bfloat16):
    drawn = scale * jax.random.normal(key, extent, jnp.float32)
    if pieces:
        drawn = drawn * steps_of(key, extent, pieces, -0.22, 0.18)
    return jnp.clip(drawn, -bound, bound).astype(held_as)


def setup_inputs(seed: int = 0, part: int = 0) -> dict:
    seeds = jax.random.split(jax.random.key(seed), 6)
    own_keys = jax.random.split(jax.random.fold_in(seeds[5], part), 6)
    return {
        "projected": gaussian(own_keys[0], (3, TOKENS, D), 1.0, 6.0, ((1, 8), (2, 2))),
        "short_filters": gaussian(seeds[1], (3, TAPS, D), 0.6, 3.0, ((2, 2),), jnp.float32),
        "decay_rate": draw_decay_rate(jax.random.fold_in(seeds[5], 71), part),
        "residue": draw_residue(jax.random.fold_in(seeds[5], 71), part),
        "skip": gaussian(seeds[4], (D,), 1.0, 4.0, ((0, 2),), jnp.float32),
    }


HIGH = lax.Precision.HIGHEST


def one_group(projected, short_filters, decay_rate, residue, skip, group_start):
    group_width = min(512, D)
    columns = lax.dynamic_slice_in_dim(projected, group_start, group_width, 2).astype(jnp.float32)
    filters = lax.dynamic_slice_in_dim(short_filters, group_start, group_width, 2)
    decay_g = lax.dynamic_slice_in_dim(decay_rate, group_start, group_width, 1)
    resid_g = lax.dynamic_slice_in_dim(residue, group_start, group_width, 1)
    skip_g = lax.dynamic_slice_in_dim(skip, group_start, group_width, 0)
    padded = jnp.pad(columns, ((0, 0), (TAPS - 1, 0), (0, 0)))
    featured = filters[:, 0, None, :] * columns
    for shift_by in range(1, TAPS):
        featured = featured + filters[:, shift_by, None, :] * padded[:, TAPS - 1 - shift_by:TAPS - 1 - shift_by + TOKENS, :]
    drive_term = featured[1] * featured[2]
    block_len = min(128, TOKENS)
    positions = jnp.arange(block_len, dtype=jnp.float32)
    offsets = jnp.arange(block_len, dtype=jnp.int32)[:, None] - jnp.arange(block_len, dtype=jnp.int32)[None, :]
    kernel = jnp.einsum("mc,nmc->nc", resid_g, jnp.exp(-decay_g[None] * positions[:, None, None]), precision=HIGH)
    toeplitz = jnp.where((offsets >= 0)[:, :, None], kernel[jnp.maximum(offsets, 0)], jnp.float32(0.0))
    into_state = jnp.exp(-decay_g[None] * (block_len - 1.0 - positions)[:, None, None])
    out_state = resid_g[None] * jnp.exp(-decay_g[None] * (positions + 1.0)[:, None, None])
    block_decay = jnp.exp(-decay_g * block_len)
    blocks = drive_term.reshape(TOKENS // block_len, block_len, group_width)

    def advance(carried, block_rows):
        conv_out = jnp.einsum("ijc,jc->ic", toeplitz, block_rows, precision=HIGH)
        conv_out = conv_out + jnp.einsum("imc,mc->ic", out_state, carried, precision=HIGH)
        carried = block_decay * carried + jnp.einsum("jmc,jc->mc", into_state, block_rows, precision=HIGH)
        return carried, conv_out

    final_state, conv_out = lax.scan(advance, jnp.zeros((MODES, group_width), jnp.float32), blocks)
    conv_out = conv_out.reshape(TOKENS, group_width)
    mixed = (featured[0] * (conv_out + skip_g[None] * drive_term)).astype(jnp.bfloat16)
    return mixed, final_state


def reference(projected, short_filters, decay_rate, residue, skip):
    group_width = min(512, D)
    group_starts = jnp.arange(D // group_width, dtype=jnp.int32) * group_width

    def per_group(group_start):
        return one_group(projected, short_filters, decay_rate, residue, skip, group_start)

    mixed, final_state = lax.map(per_group, group_starts)
    mixed = jnp.transpose(mixed, (1, 0, 2)).reshape(TOKENS, D)
    final_state = jnp.transpose(final_state, (1, 0, 2)).reshape(MODES, D)
    return mixed, final_state
```

```python
import functools

import jax
import jax.numpy as jnp
from jax import lax
from jax.experimental import pallas as pl
from jax.experimental.pallas import tpu as pltpu
from jax.sharding import PartitionSpec as P

CHAN_BLOCK = 512
ROW_GROUP = 8


def from_behind(value, axis, steps):
    count = lax.axis_size(axis)
    initial, last = (max(0, -steps), min(count, count - steps))
    return lax.ppermute(value, axis, [(source, source + steps) for source in range(initial, last)])


def _featurize_one(x_ref, halo_ref, filt_ref, index):
    x = x_ref[index].astype(jnp.float32)
    halo = halo_ref[index].astype(jnp.float32)
    taps = filt_ref[index]
    rows = lax.broadcasted_iota(jnp.int32, x.shape, 0)
    last = halo[halo.shape[0] - 1 : halo.shape[0]]
    second = halo[halo.shape[0] - 2 : halo.shape[0] - 1]
    back1 = jnp.where(rows == 0, last, pltpu.roll(x, 1, 0))
    back2 = jnp.where(rows == 0, second, jnp.where(rows == 1, last, pltpu.roll(x, 2, 0)))
    return taps[0:1] * x + taps[1:2] * back1 + taps[2:3] * back2


def _scan_rows(drive_ref, decay, residue, state, conv_ref):
    row_count = drive_ref.shape[0]
    modes = state.shape[0]

    def body(group, state):
        start = pl.multiple_of(group * ROW_GROUP, ROW_GROUP)
        rows = []
        block = drive_ref[pl.ds(start, ROW_GROUP), :]
        for i in range(ROW_GROUP):
            drive_row = jnp.broadcast_to(block[i : i + 1], state.shape)
            state = decay * state + drive_row
            if conv_ref is not None:
                rows.append(jnp.sum(residue * state, axis=0, keepdims=True))
        if conv_ref is not None:
            conv_ref[pl.ds(start, ROW_GROUP), :] = jnp.concatenate(rows, axis=0)
        return state

    return lax.fori_loop(0, row_count // ROW_GROUP, body, state)


def _contrib_kernel(x_ref, halo_ref, filt_ref, rate_ref, out_ref, drive_scr):
    k = _featurize_one(x_ref, halo_ref, filt_ref, 1)
    v = _featurize_one(x_ref, halo_ref, filt_ref, 2)
    drive_scr[...] = k * v
    decay = jnp.exp(-rate_ref[...])
    state = jnp.zeros(out_ref.shape, jnp.float32)
    out_ref[...] = _scan_rows(drive_scr, decay, None, state, None)


def _mix_kernel(x_ref, halo_ref, filt_ref, rate_ref, res_ref, skip_ref, init_ref, out_ref,
                drive_scr, conv_scr):
    k = _featurize_one(x_ref, halo_ref, filt_ref, 1)
    v = _featurize_one(x_ref, halo_ref, filt_ref, 2)
    drive = k * v
    drive_scr[...] = drive
    decay = jnp.exp(-rate_ref[...])
    _scan_rows(drive_scr, decay, res_ref[...], init_ref[...], conv_scr)
    q = _featurize_one(x_ref, halo_ref, filt_ref, 0)
    out_ref[...] = (q * (conv_scr[...] + skip_ref[...] * drive_scr[...])).astype(out_ref.dtype)


def _specs(row_count, modes, taps):
    x_spec = pl.BlockSpec((3, row_count, CHAN_BLOCK), lambda j: (0, 0, j))
    halo_spec = pl.BlockSpec((3, taps - 1, CHAN_BLOCK), lambda j: (0, 0, j))
    filt_spec = pl.BlockSpec((3, taps, CHAN_BLOCK), lambda j: (0, 0, j))
    mode_spec = pl.BlockSpec((modes, CHAN_BLOCK), lambda j: (0, j))
    row_spec = pl.BlockSpec((1, CHAN_BLOCK), lambda j: (0, j))
    return x_spec, halo_spec, filt_spec, mode_spec, row_spec


def contributions(projected, halo, short_filters, decay_rate):
    _, row_count, chan_count = projected.shape
    modes = decay_rate.shape[0]
    taps = short_filters.shape[1]
    x_spec, halo_spec, filt_spec, mode_spec, _ = _specs(row_count, modes, taps)
    return pl.pallas_call(
        _contrib_kernel,
        grid=(chan_count // CHAN_BLOCK,),
        in_specs=[x_spec, halo_spec, filt_spec, mode_spec],
        out_specs=mode_spec,
        out_shape=jax.ShapeDtypeStruct((modes, chan_count), jnp.float32),
        scratch_shapes=[pltpu.VMEM((row_count, CHAN_BLOCK), jnp.float32)],
    )(projected, halo, short_filters, decay_rate)


def mix(projected, halo, short_filters, decay_rate, residue, skip, prefix):
    _, row_count, chan_count = projected.shape
    modes = decay_rate.shape[0]
    taps = short_filters.shape[1]
    x_spec, halo_spec, filt_spec, mode_spec, row_spec = _specs(row_count, modes, taps)
    return pl.pallas_call(
        _mix_kernel,
        grid=(chan_count // CHAN_BLOCK,),
        in_specs=[x_spec, halo_spec, filt_spec, mode_spec, mode_spec, row_spec, mode_spec],
        out_specs=pl.BlockSpec((row_count, CHAN_BLOCK), lambda j: (0, j)),
        out_shape=jax.ShapeDtypeStruct((row_count, chan_count), jnp.bfloat16),
        scratch_shapes=[
            pltpu.VMEM((row_count, CHAN_BLOCK), jnp.float32),
            pltpu.VMEM((row_count, CHAN_BLOCK), jnp.float32),
        ],
    )(projected, halo, short_filters, decay_rate, residue, skip[None, :], prefix)


def local(projected, short_filters, decay_rate, residue, skip):
    tap_count = short_filters.shape[1]
    row_count = projected.shape[1]
    edge_rows = projected[:, row_count - (tap_count - 1) :, :]
    halo = from_behind(edge_rows, ("ctx", "dec"), 1)
    contribution = contributions(projected, halo, short_filters, decay_rate)
    received = lax.all_gather(contribution, ("ctx", "dec"), axis=0, tiled=False)
    rank_here = lax.axis_index(("ctx", "dec"))
    shard_decay = jnp.exp(-decay_rate * row_count)
    running = jnp.zeros_like(contribution)
    prefix = jnp.zeros_like(contribution)
    for shard in range(received.shape[0]):
        prefix = jnp.where(rank_here == shard, running, prefix)
        running = shard_decay * running + received[shard]
    mixed = mix(projected, halo, short_filters, decay_rate, residue, skip, prefix)
    return (mixed, running)


def solution(mesh):
    placed = (
        P(None, ("grp", "ctx", "dec"), "chan"),
        P(None, None, "chan"),
        P(None, "chan"),
        P(None, "chan"),
        P("chan"),
    )
    return jax.shard_map(
        local,
        mesh=mesh,
        in_specs=placed,
        out_specs=(P(("grp", "ctx", "dec"), "chan"), P("grp", "chan")),
        check_vma=False,
    )
```

```python
import functools

import jax
import jax.numpy as jnp
from jax import lax
from jax.experimental import pallas as pl
from jax.experimental.pallas import tpu as pltpu
from jax.sharding import PartitionSpec as P

CHAN_BLOCK = 512
ROW_GROUP = 8


def from_behind(value, axis, steps):
    count = lax.axis_size(axis)
    initial, last = (max(0, -steps), min(count, count - steps))
    return lax.ppermute(value, axis, [(source, source + steps) for source in range(initial, last)])


def _featurize_one(x_ref, halo_ref, filt_ref, index):
    x = x_ref[index].astype(jnp.float32)
    halo = halo_ref[index].astype(jnp.float32)
    taps = filt_ref[index]
    rows = lax.broadcasted_iota(jnp.int32, x.shape, 0)
    last = halo[halo.shape[0] - 1 : halo.shape[0]]
    second = halo[halo.shape[0] - 2 : halo.shape[0] - 1]
    back1 = jnp.where(rows == 0, last, pltpu.roll(x, 1, 0))
    back2 = jnp.where(rows == 0, second, jnp.where(rows == 1, last, pltpu.roll(x, 2, 0)))
    return taps[0:1] * x + taps[1:2] * back1 + taps[2:3] * back2


def _scan_rows(drive_ref, decay, residue, state, conv_ref):
    row_count = drive_ref.shape[0]
    modes = state.shape[0]

    def body(group, state):
        start = pl.multiple_of(group * ROW_GROUP, ROW_GROUP)
        rows = []
        block = drive_ref[pl.ds(start, ROW_GROUP), :]
        for i in range(ROW_GROUP):
            drive_row = jnp.broadcast_to(block[i : i + 1], state.shape)
            state = decay * state + drive_row
            if conv_ref is not None:
                rows.append(jnp.sum(residue * state, axis=0, keepdims=True))
        if conv_ref is not None:
            conv_ref[pl.ds(start, ROW_GROUP), :] = jnp.concatenate(rows, axis=0)
        return state

    return lax.fori_loop(0, row_count // ROW_GROUP, body, state)


def _contrib_kernel(x_ref, halo_ref, filt_ref, rate_ref, out_ref, drive_scr):
    k = _featurize_one(x_ref, halo_ref, filt_ref, 1)
    v = _featurize_one(x_ref, halo_ref, filt_ref, 2)
    drive_scr[...] = k * v
    decay = jnp.exp(-rate_ref[...])
    state = jnp.zeros(out_ref.shape, jnp.float32)
    out_ref[...] = _scan_rows(drive_scr, decay, None, state, None)


def _mix_kernel(x_ref, halo_ref, filt_ref, rate_ref, res_ref, skip_ref, init_ref, out_ref,
                drive_scr, conv_scr):
    k = _featurize_one(x_ref, halo_ref, filt_ref, 1)
    v = _featurize_one(x_ref, halo_ref, filt_ref, 2)
    drive = k * v
    drive_scr[...] = drive
    decay = jnp.exp(-rate_ref[...])
    _scan_rows(drive_scr, decay, res_ref[...], init_ref[...], conv_scr)
    q = _featurize_one(x_ref, halo_ref, filt_ref, 0)
    out_ref[...] = (q * (conv_scr[...] + skip_ref[...] * drive_scr[...])).astype(out_ref.dtype)


def _specs(row_count, modes, taps):
    x_spec = pl.BlockSpec((3, row_count, CHAN_BLOCK), lambda j: (0, 0, j))
    halo_spec = pl.BlockSpec((3, taps - 1, CHAN_BLOCK), lambda j: (0, 0, j))
    filt_spec = pl.BlockSpec((3, taps, CHAN_BLOCK), lambda j: (0, 0, j))
    mode_spec = pl.BlockSpec((modes, CHAN_BLOCK), lambda j: (0, j))
    row_spec = pl.BlockSpec((1, CHAN_BLOCK), lambda j: (0, j))
    return x_spec, halo_spec, filt_spec, mode_spec, row_spec


def contributions(projected, halo, short_filters, decay_rate):
    _, row_count, chan_count = projected.shape
    modes = decay_rate.shape[0]
    taps = short_filters.shape[1]
    x_spec, halo_spec, filt_spec, mode_spec, _ = _specs(row_count, modes, taps)
    return pl.pallas_call(
        _contrib_kernel,
        grid=(chan_count // CHAN_BLOCK,),
        in_specs=[x_spec, halo_spec, filt_spec, mode_spec],
        out_specs=mode_spec,
        out_shape=jax.ShapeDtypeStruct((modes, chan_count), jnp.float32),
        scratch_shapes=[pltpu.VMEM((row_count, CHAN_BLOCK), jnp.float32)],
    )(projected, halo, short_filters, decay_rate)


def mix(projected, halo, short_filters, decay_rate, residue, skip, prefix):
    _, row_count, chan_count = projected.shape
    modes = decay_rate.shape[0]
    taps = short_filters.shape[1]
    x_spec, halo_spec, filt_spec, mode_spec, row_spec = _specs(row_count, modes, taps)
    return pl.pallas_call(
        _mix_kernel,
        grid=(chan_count // CHAN_BLOCK,),
        in_specs=[x_spec, halo_spec, filt_spec, mode_spec, mode_spec, row_spec, mode_spec],
        out_specs=pl.BlockSpec((row_count, CHAN_BLOCK), lambda j: (0, j)),
        out_shape=jax.ShapeDtypeStruct((row_count, chan_count), jnp.bfloat16),
        scratch_shapes=[
            pltpu.VMEM((row_count, CHAN_BLOCK), jnp.float32),
            pltpu.VMEM((row_count, CHAN_BLOCK), jnp.float32),
        ],
    )(projected, halo, short_filters, decay_rate, residue, skip[None, :], prefix)


def swap_cores(value):
    return lax.ppermute(value, "dec", [(0, 1), (1, 0)])


def local(projected, short_filters, decay_rate, residue, skip):
    tap_count = short_filters.shape[1]
    row_count = projected.shape[1]
    chan_count = projected.shape[2]
    edge_rows = projected[:, row_count - (tap_count - 1) :, :]
    halo = from_behind(edge_rows, ("ctx", "dec"), 1)
    contribution = contributions(projected, halo, short_filters, decay_rate)
    core = lax.axis_index("dec")
    other = swap_cores(contribution)
    first_core = jnp.where(core == 0, contribution, other)
    second_core = jnp.where(core == 0, other, contribution)
    shard_decay = jnp.exp(-decay_rate * row_count)
    half = chan_count // 2
    start = core * half
    mine = lambda x: lax.dynamic_slice_in_dim(x, start, half, 1)
    chip_decay = mine(shard_decay) * mine(shard_decay)
    chip_part = mine(shard_decay) * mine(first_core) + mine(second_core)
    received = lax.all_gather(chip_part, "ctx", axis=0, tiled=False)
    chip_here = lax.axis_index("ctx")
    running = jnp.zeros_like(chip_part)
    entering = jnp.zeros_like(chip_part)
    for chip in range(received.shape[0]):
        entering = jnp.where(chip_here == chip, running, entering)
        running = chip_decay * running + received[chip]
    both = jnp.concatenate([entering, running], axis=0)
    other_both = swap_cores(both)
    low = jnp.where(core == 0, both, other_both)
    high = jnp.where(core == 0, other_both, both)
    whole = jnp.concatenate([low, high], axis=1)
    modes = decay_rate.shape[0]
    chip_entering = whole[:modes]
    final_state = whole[modes:]
    prefix = jnp.where(core == 0, chip_entering, shard_decay * chip_entering + first_core)
    mixed = mix(projected, halo, short_filters, decay_rate, residue, skip, prefix)
    return (mixed, final_state)


def solution(mesh):
    placed = (
        P(None, ("grp", "ctx", "dec"), "chan"),
        P(None, None, "chan"),
        P(None, "chan"),
        P(None, "chan"),
        P("chan"),
    )
    return jax.shard_map(
        local,
        mesh=mesh,
        in_specs=placed,
        out_specs=(P(("grp", "ctx", "dec"), "chan"), P("grp", "chan")),
        check_vma=False,
    )
```

```python
import functools

import jax
import jax.numpy as jnp
from jax import lax
from jax.experimental import pallas as pl
from jax.experimental.pallas import tpu as pltpu
from jax.sharding import PartitionSpec as P

CHAN_BLOCK = 512
ROW_GROUP = 8


def from_behind(value, axis, steps):
    count = lax.axis_size(axis)
    initial, last = (max(0, -steps), min(count, count - steps))
    return lax.ppermute(value, axis, [(source, source + steps) for source in range(initial, last)])


def _featurize_one(x_ref, halo_ref, filt_ref, index):
    x = x_ref[index].astype(jnp.float32)
    halo = halo_ref[index].astype(jnp.float32)
    taps = filt_ref[index]
    rows = lax.broadcasted_iota(jnp.int32, x.shape, 0)
    last = halo[halo.shape[0] - 1 : halo.shape[0]]
    second = halo[halo.shape[0] - 2 : halo.shape[0] - 1]
    back1 = jnp.where(rows == 0, last, pltpu.roll(x, 1, 0))
    back2 = jnp.where(rows == 0, second, jnp.where(rows == 1, last, pltpu.roll(x, 2, 0)))
    return taps[0:1] * x + taps[1:2] * back1 + taps[2:3] * back2


def _scan_rows(drive_ref, decay, residue, state, conv_ref):
    row_count = drive_ref.shape[0]
    modes = state.shape[0]

    def body(group, state):
        start = pl.multiple_of(group * ROW_GROUP, ROW_GROUP)
        rows = []
        block = drive_ref[pl.ds(start, ROW_GROUP), :]
        for i in range(ROW_GROUP):
            drive_row = jnp.broadcast_to(block[i : i + 1], state.shape)
            state = decay * state + drive_row
            if conv_ref is not None:
                rows.append(jnp.sum(residue * state, axis=0, keepdims=True))
        if conv_ref is not None:
            conv_ref[pl.ds(start, ROW_GROUP), :] = jnp.concatenate(rows, axis=0)
        return state

    return lax.fori_loop(0, row_count // ROW_GROUP, body, state)


def _contrib_kernel(x_ref, halo_ref, filt_ref, rate_ref, out_ref, drive_scr):
    k = _featurize_one(x_ref, halo_ref, filt_ref, 1)
    v = _featurize_one(x_ref, halo_ref, filt_ref, 2)
    drive_scr[...] = k * v
    decay = jnp.exp(-rate_ref[...])
    state = jnp.zeros(out_ref.shape, jnp.float32)
    out_ref[...] = _scan_rows(drive_scr, decay, None, state, None)


def _mix_kernel(x_ref, halo_ref, filt_ref, rate_ref, res_ref, skip_ref, init_ref, out_ref,
                drive_scr, conv_scr):
    k = _featurize_one(x_ref, halo_ref, filt_ref, 1)
    v = _featurize_one(x_ref, halo_ref, filt_ref, 2)
    drive = k * v
    drive_scr[...] = drive
    decay = jnp.exp(-rate_ref[...])
    _scan_rows(drive_scr, decay, res_ref[...], init_ref[...], conv_scr)
    q = _featurize_one(x_ref, halo_ref, filt_ref, 0)
    out_ref[...] = (q * (conv_scr[...] + skip_ref[...] * drive_scr[...])).astype(out_ref.dtype)


def _specs(row_count, modes, taps):
    x_spec = pl.BlockSpec((3, row_count, CHAN_BLOCK), lambda j: (0, 0, j))
    halo_spec = pl.BlockSpec((3, taps - 1, CHAN_BLOCK), lambda j: (0, 0, j))
    filt_spec = pl.BlockSpec((3, taps, CHAN_BLOCK), lambda j: (0, 0, j))
    mode_spec = pl.BlockSpec((modes, CHAN_BLOCK), lambda j: (0, j))
    row_spec = pl.BlockSpec((1, CHAN_BLOCK), lambda j: (0, j))
    return x_spec, halo_spec, filt_spec, mode_spec, row_spec


def contributions(projected, halo, short_filters, decay_rate):
    _, row_count, chan_count = projected.shape
    modes = decay_rate.shape[0]
    taps = short_filters.shape[1]
    x_spec, halo_spec, filt_spec, mode_spec, _ = _specs(row_count, modes, taps)
    return pl.pallas_call(
        _contrib_kernel,
        grid=(chan_count // CHAN_BLOCK,),
        in_specs=[x_spec, halo_spec, filt_spec, mode_spec],
        out_specs=mode_spec,
        out_shape=jax.ShapeDtypeStruct((modes, chan_count), jnp.float32),
        scratch_shapes=[pltpu.VMEM((row_count, CHAN_BLOCK), jnp.float32)],
    )(projected, halo, short_filters, decay_rate)


def mix(projected, halo, short_filters, decay_rate, residue, skip, prefix):
    _, row_count, chan_count = projected.shape
    modes = decay_rate.shape[0]
    taps = short_filters.shape[1]
    x_spec, halo_spec, filt_spec, mode_spec, row_spec = _specs(row_count, modes, taps)
    return pl.pallas_call(
        _mix_kernel,
        grid=(chan_count // CHAN_BLOCK,),
        in_specs=[x_spec, halo_spec, filt_spec, mode_spec, mode_spec, row_spec, mode_spec],
        out_specs=pl.BlockSpec((row_count, CHAN_BLOCK), lambda j: (0, j)),
        out_shape=jax.ShapeDtypeStruct((row_count, chan_count), jnp.bfloat16),
        scratch_shapes=[
            pltpu.VMEM((row_count, CHAN_BLOCK), jnp.float32),
            pltpu.VMEM((row_count, CHAN_BLOCK), jnp.float32),
        ],
    )(projected, halo, short_filters, decay_rate, residue, skip[None, :], prefix)


def swap_cores(value):
    return lax.ppermute(value, "dec", [(0, 1), (1, 0)])


def local(projected, short_filters, decay_rate, residue, skip):
    tap_count = short_filters.shape[1]
    row_count = projected.shape[1]
    chan_count = projected.shape[2]
    edge_rows = projected[:, row_count - (tap_count - 1) :, :]
    halo = from_behind(edge_rows, ("ctx", "dec"), 1)
    contribution = contributions(projected, halo, short_filters, decay_rate)
    core = lax.axis_index("dec")
    other = swap_cores(contribution)
    first_core = jnp.where(core == 0, contribution, other)
    second_core = jnp.where(core == 0, other, contribution)
    shard_decay = jnp.exp(-decay_rate * row_count)
    half = chan_count // 2
    start = core * half
    mine = lambda x: lax.dynamic_slice_in_dim(x, start, half, 1)
    chip_decay = mine(shard_decay) * mine(shard_decay)
    chip_part = mine(shard_decay) * mine(first_core) + mine(second_core)
    chip_here = lax.axis_index("ctx")
    chips = lax.axis_size("ctx")
    ahead = [from_behind(chip_part, "ctx", k) for k in range(1, chips)]
    behind = [from_behind(chip_part, "ctx", -k) for k in range(1, chips)]
    running = jnp.zeros_like(chip_part)
    entering = jnp.zeros_like(chip_part)
    for chip in range(chips):
        part = chip_part
        for k in range(1, chips):
            part = jnp.where(chip_here - k == chip, ahead[k - 1], part)
            part = jnp.where(chip_here + k == chip, behind[k - 1], part)
        entering = jnp.where(chip_here == chip, running, entering)
        running = chip_decay * running + part
    both = jnp.concatenate([entering, running], axis=0)
    other_both = swap_cores(both)
    low = jnp.where(core == 0, both, other_both)
    high = jnp.where(core == 0, other_both, both)
    whole = jnp.concatenate([low, high], axis=1)
    modes = decay_rate.shape[0]
    chip_entering = whole[:modes]
    final_state = whole[modes:]
    prefix = jnp.where(core == 0, chip_entering, shard_decay * chip_entering + first_core)
    mixed = mix(projected, halo, short_filters, decay_rate, residue, skip, prefix)
    return (mixed, final_state)


def solution(mesh):
    placed = (
        P(None, ("grp", "ctx", "dec"), "chan"),
        P(None, None, "chan"),
        P(None, "chan"),
        P(None, "chan"),
        P("chan"),
    )
    return jax.shard_map(
        local,
        mesh=mesh,
        in_specs=placed,
        out_specs=(P(("grp", "ctx", "dec"), "chan"), P("grp", "chan")),
        check_vma=False,
    )
```

```python
import functools

import jax
import jax.numpy as jnp
from jax import lax
from jax.experimental import pallas as pl
from jax.experimental.pallas import tpu as pltpu
from jax.sharding import PartitionSpec as P

CHAN_BLOCK = 512
ROW_GROUP = 8


def from_behind(value, axis, steps):
    count = lax.axis_size(axis)
    initial, last = (max(0, -steps), min(count, count - steps))
    return lax.ppermute(value, axis, [(source, source + steps) for source in range(initial, last)])


def _featurize_one(x_ref, halo_ref, filt_ref, index):
    x = x_ref[index].astype(jnp.float32)
    halo = halo_ref[index].astype(jnp.float32)
    taps = filt_ref[index]
    rows = lax.broadcasted_iota(jnp.int32, x.shape, 0)
    last = halo[halo.shape[0] - 1 : halo.shape[0]]
    second = halo[halo.shape[0] - 2 : halo.shape[0] - 1]
    back1 = jnp.where(rows == 0, last, pltpu.roll(x, 1, 0))
    back2 = jnp.where(rows == 0, second, jnp.where(rows == 1, last, pltpu.roll(x, 2, 0)))
    return taps[0:1] * x + taps[1:2] * back1 + taps[2:3] * back2


def _scan_rows(drive_ref, decay, residue, state, conv_ref):
    row_count = drive_ref.shape[0]
    modes = state.shape[0]

    def body(group, state):
        start = pl.multiple_of(group * ROW_GROUP, ROW_GROUP)
        rows = []
        block = drive_ref[pl.ds(start, ROW_GROUP), :]
        for i in range(ROW_GROUP):
            drive_row = jnp.broadcast_to(block[i : i + 1], state.shape)
            state = decay * state + drive_row
            if conv_ref is not None:
                rows.append(jnp.sum(residue * state, axis=0, keepdims=True))
        if conv_ref is not None:
            conv_ref[pl.ds(start, ROW_GROUP), :] = jnp.concatenate(rows, axis=0)
        return state

    return lax.fori_loop(0, row_count // ROW_GROUP, body, state)


def _contrib_kernel(x_ref, halo_ref, filt_ref, rate_ref, out_ref, drive_scr):
    k = _featurize_one(x_ref, halo_ref, filt_ref, 1)
    v = _featurize_one(x_ref, halo_ref, filt_ref, 2)
    drive_scr[...] = k * v
    decay = jnp.exp(-rate_ref[...])
    state = jnp.zeros(out_ref.shape, jnp.float32)
    out_ref[...] = _scan_rows(drive_scr, decay, None, state, None)


def _local_kernel(x_ref, halo_ref, filt_ref, rate_ref, res_ref, skip_ref, out_ref, drive_scr):
    k = _featurize_one(x_ref, halo_ref, filt_ref, 1)
    v = _featurize_one(x_ref, halo_ref, filt_ref, 2)
    drive_scr[...] = k * v
    decay = jnp.exp(-rate_ref[...])
    state = jnp.zeros(rate_ref.shape, jnp.float32)
    _scan_rows(drive_scr, decay, res_ref[...], state, out_ref)
    out_ref[...] = out_ref[...] + skip_ref[...] * drive_scr[...]


def _finish_kernel(x_ref, halo_ref, filt_ref, rate_ref, res_ref, init_ref, local_ref, out_ref,
                   corr_scr):
    modes, chan_block = rate_ref.shape
    row_count = local_ref.shape[0]
    lanes = 128
    steps = lax.broadcasted_iota(jnp.int32, (ROW_GROUP, lanes), 0).astype(jnp.float32) + 1.0
    for group in range(chan_block // lanes):
        cols = slice(group * lanes, (group + 1) * lanes)
        rate = rate_ref[:, cols]
        weight = res_ref[:, cols] * init_ref[:, cols]
        terms = []
        jumps = []
        for m in range(modes):
            rate_m = jnp.broadcast_to(rate[m : m + 1], (ROW_GROUP, lanes))
            terms.append(jnp.broadcast_to(weight[m : m + 1], (ROW_GROUP, lanes)) * jnp.exp(-rate_m * steps))
            jumps.append(jnp.exp(-rate_m * float(ROW_GROUP)))

        def body(block, terms):
            start = pl.multiple_of(block * ROW_GROUP, ROW_GROUP)
            total = terms[0]
            for m in range(1, modes):
                total = total + terms[m]
            corr_scr[pl.ds(start, ROW_GROUP), cols] = total
            return tuple(terms[m] * jumps[m] for m in range(modes))

        lax.fori_loop(0, row_count // ROW_GROUP, body, tuple(terms))
    q = _featurize_one(x_ref, halo_ref, filt_ref, 0)
    out_ref[...] = (q * (local_ref[...] + corr_scr[...])).astype(out_ref.dtype)


def _specs(row_count, modes, taps):
    x_spec = pl.BlockSpec((3, row_count, CHAN_BLOCK), lambda j: (0, 0, j))
    halo_spec = pl.BlockSpec((3, taps - 1, CHAN_BLOCK), lambda j: (0, 0, j))
    filt_spec = pl.BlockSpec((3, taps, CHAN_BLOCK), lambda j: (0, 0, j))
    mode_spec = pl.BlockSpec((modes, CHAN_BLOCK), lambda j: (0, j))
    row_spec = pl.BlockSpec((1, CHAN_BLOCK), lambda j: (0, j))
    return x_spec, halo_spec, filt_spec, mode_spec, row_spec


def contributions(projected, halo, short_filters, decay_rate):
    _, row_count, chan_count = projected.shape
    modes = decay_rate.shape[0]
    taps = short_filters.shape[1]
    x_spec, halo_spec, filt_spec, mode_spec, _ = _specs(row_count, modes, taps)
    return pl.pallas_call(
        _contrib_kernel,
        grid=(chan_count // CHAN_BLOCK,),
        in_specs=[x_spec, halo_spec, filt_spec, mode_spec],
        out_specs=mode_spec,
        out_shape=jax.ShapeDtypeStruct((modes, chan_count), jnp.float32),
        scratch_shapes=[pltpu.VMEM((row_count, CHAN_BLOCK), jnp.float32)],
    )(projected, halo, short_filters, decay_rate)


def local_scan(projected, halo, short_filters, decay_rate, residue, skip):
    _, row_count, chan_count = projected.shape
    modes = decay_rate.shape[0]
    taps = short_filters.shape[1]
    x_spec, halo_spec, filt_spec, mode_spec, row_spec = _specs(row_count, modes, taps)
    return pl.pallas_call(
        _local_kernel,
        grid=(chan_count // CHAN_BLOCK,),
        in_specs=[x_spec, halo_spec, filt_spec, mode_spec, mode_spec, row_spec],
        out_specs=pl.BlockSpec((row_count, CHAN_BLOCK), lambda j: (0, j)),
        out_shape=jax.ShapeDtypeStruct((row_count, chan_count), jnp.float32),
        scratch_shapes=[pltpu.VMEM((row_count, CHAN_BLOCK), jnp.float32)],
    )(projected, halo, short_filters, decay_rate, residue, skip[None, :])


def finish(projected, halo, short_filters, decay_rate, residue, prefix, local_part):
    _, row_count, chan_count = projected.shape
    modes = decay_rate.shape[0]
    taps = short_filters.shape[1]
    x_spec, halo_spec, filt_spec, mode_spec, _ = _specs(row_count, modes, taps)
    tile_spec = pl.BlockSpec((row_count, CHAN_BLOCK), lambda j: (0, j))
    return pl.pallas_call(
        _finish_kernel,
        grid=(chan_count // CHAN_BLOCK,),
        in_specs=[x_spec, halo_spec, filt_spec, mode_spec, mode_spec, mode_spec, tile_spec],
        out_specs=tile_spec,
        out_shape=jax.ShapeDtypeStruct((row_count, chan_count), jnp.bfloat16),
        scratch_shapes=[pltpu.VMEM((row_count, CHAN_BLOCK), jnp.float32)],
    )(projected, halo, short_filters, decay_rate, residue, prefix, local_part)


def swap_cores(value):
    return lax.ppermute(value, "dec", [(0, 1), (1, 0)])


def local(projected, short_filters, decay_rate, residue, skip):
    tap_count = short_filters.shape[1]
    row_count = projected.shape[1]
    chan_count = projected.shape[2]
    edge_rows = projected[:, row_count - (tap_count - 1) :, :]
    halo = from_behind(edge_rows, ("ctx", "dec"), 1)
    contribution = contributions(projected, halo, short_filters, decay_rate)
    core = lax.axis_index("dec")
    other = swap_cores(contribution)
    first_core = jnp.where(core == 0, contribution, other)
    second_core = jnp.where(core == 0, other, contribution)
    shard_decay = jnp.exp(-decay_rate * row_count)
    half = chan_count // 2
    start = core * half
    mine = lambda x: lax.dynamic_slice_in_dim(x, start, half, 1)
    chip_part = mine(shard_decay) * mine(first_core) + mine(second_core)
    received = lax.all_gather(chip_part, ("ctx", "dec"), axis=0, tiled=False)
    local_part = local_scan(projected, halo, short_filters, decay_rate, residue, skip)
    chip_here = lax.axis_index("ctx")
    chip_decay = shard_decay * shard_decay
    running = jnp.zeros_like(contribution)
    entering = jnp.zeros_like(contribution)
    for chip in range(received.shape[0] // 2):
        part = jnp.concatenate([received[2 * chip], received[2 * chip + 1]], axis=1)
        entering = jnp.where(chip_here == chip, running, entering)
        running = chip_decay * running + part
    prefix = jnp.where(core == 0, entering, shard_decay * entering + first_core)
    mixed = finish(projected, halo, short_filters, decay_rate, residue, prefix, local_part)
    return (mixed, running)


def solution(mesh):
    placed = (
        P(None, ("grp", "ctx", "dec"), "chan"),
        P(None, None, "chan"),
        P(None, "chan"),
        P(None, "chan"),
        P("chan"),
    )
    return jax.shard_map(
        local,
        mesh=mesh,
        in_specs=placed,
        out_specs=(P(("grp", "ctx", "dec"), "chan"), P("grp", "chan")),
        check_vma=False,
    )
```

```python
import functools

import jax
import jax.numpy as jnp
from jax import lax
from jax.experimental import pallas as pl
from jax.experimental.pallas import tpu as pltpu
from jax.sharding import PartitionSpec as P

CHAN_BLOCK = 512
ROW_GROUP = 8


def from_behind(value, axis, steps):
    count = lax.axis_size(axis)
    initial, last = (max(0, -steps), min(count, count - steps))
    return lax.ppermute(value, axis, [(source, source + steps) for source in range(initial, last)])


def _featurize_one(x_ref, halo_ref, filt_ref, index):
    x = x_ref[index].astype(jnp.float32)
    halo = halo_ref[index].astype(jnp.float32)
    taps = filt_ref[index]
    rows = lax.broadcasted_iota(jnp.int32, x.shape, 0)
    last = halo[halo.shape[0] - 1 : halo.shape[0]]
    second = halo[halo.shape[0] - 2 : halo.shape[0] - 1]
    back1 = jnp.where(rows == 0, last, pltpu.roll(x, 1, 0))
    back2 = jnp.where(rows == 0, second, jnp.where(rows == 1, last, pltpu.roll(x, 2, 0)))
    return taps[0:1] * x + taps[1:2] * back1 + taps[2:3] * back2


def _scan_rows(drive_ref, decay, residue, state, conv_ref):
    row_count = drive_ref.shape[0]
    modes = state.shape[0]

    def body(group, state):
        start = pl.multiple_of(group * ROW_GROUP, ROW_GROUP)
        rows = []
        block = drive_ref[pl.ds(start, ROW_GROUP), :]
        for i in range(ROW_GROUP):
            drive_row = jnp.broadcast_to(block[i : i + 1], state.shape)
            state = decay * state + drive_row
            if conv_ref is not None:
                rows.append(jnp.sum(residue * state, axis=0, keepdims=True))
        if conv_ref is not None:
            conv_ref[pl.ds(start, ROW_GROUP), :] = jnp.concatenate(rows, axis=0)
        return state

    return lax.fori_loop(0, row_count // ROW_GROUP, body, state)


def _contrib_kernel(x_ref, halo_ref, filt_ref, rate_ref, out_ref, drive_scr):
    k = _featurize_one(x_ref, halo_ref, filt_ref, 1)
    v = _featurize_one(x_ref, halo_ref, filt_ref, 2)
    drive_scr[...] = k * v
    decay = jnp.exp(-rate_ref[...])
    state = jnp.zeros(out_ref.shape, jnp.float32)
    out_ref[...] = _scan_rows(drive_scr, decay, None, state, None)


def _mix_kernel(x_ref, halo_ref, filt_ref, rate_ref, res_ref, skip_ref, init_ref, out_ref,
                drive_scr, conv_scr):
    k = _featurize_one(x_ref, halo_ref, filt_ref, 1)
    v = _featurize_one(x_ref, halo_ref, filt_ref, 2)
    drive = k * v
    drive_scr[...] = drive
    decay = jnp.exp(-rate_ref[...])
    _scan_rows(drive_scr, decay, res_ref[...], init_ref[...], conv_scr)
    q = _featurize_one(x_ref, halo_ref, filt_ref, 0)
    out_ref[...] = (q * (conv_scr[...] + skip_ref[...] * drive_scr[...])).astype(out_ref.dtype)


def _specs(row_count, modes, taps):
    x_spec = pl.BlockSpec((3, row_count, CHAN_BLOCK), lambda j: (0, 0, j))
    halo_spec = pl.BlockSpec((3, taps - 1, CHAN_BLOCK), lambda j: (0, 0, j))
    filt_spec = pl.BlockSpec((3, taps, CHAN_BLOCK), lambda j: (0, 0, j))
    mode_spec = pl.BlockSpec((modes, CHAN_BLOCK), lambda j: (0, j))
    row_spec = pl.BlockSpec((1, CHAN_BLOCK), lambda j: (0, j))
    return x_spec, halo_spec, filt_spec, mode_spec, row_spec


def contributions(projected, halo, short_filters, decay_rate):
    _, row_count, chan_count = projected.shape
    modes = decay_rate.shape[0]
    taps = short_filters.shape[1]
    x_spec, halo_spec, filt_spec, mode_spec, _ = _specs(row_count, modes, taps)
    return pl.pallas_call(
        _contrib_kernel,
        grid=(chan_count // CHAN_BLOCK,),
        in_specs=[x_spec, halo_spec, filt_spec, mode_spec],
        out_specs=mode_spec,
        out_shape=jax.ShapeDtypeStruct((modes, chan_count), jnp.float32),
        scratch_shapes=[pltpu.VMEM((row_count, CHAN_BLOCK), jnp.float32)],
    )(projected, halo, short_filters, decay_rate)


def mix(projected, halo, short_filters, decay_rate, residue, skip, prefix):
    _, row_count, chan_count = projected.shape
    modes = decay_rate.shape[0]
    taps = short_filters.shape[1]
    x_spec, halo_spec, filt_spec, mode_spec, row_spec = _specs(row_count, modes, taps)
    return pl.pallas_call(
        _mix_kernel,
        grid=(chan_count // CHAN_BLOCK,),
        in_specs=[x_spec, halo_spec, filt_spec, mode_spec, mode_spec, row_spec, mode_spec],
        out_specs=pl.BlockSpec((row_count, CHAN_BLOCK), lambda j: (0, j)),
        out_shape=jax.ShapeDtypeStruct((row_count, chan_count), jnp.bfloat16),
        scratch_shapes=[
            pltpu.VMEM((row_count, CHAN_BLOCK), jnp.float32),
            pltpu.VMEM((row_count, CHAN_BLOCK), jnp.float32),
        ],
    )(projected, halo, short_filters, decay_rate, residue, skip[None, :], prefix)


def swap_cores(value):
    return lax.ppermute(value, "dec", [(0, 1), (1, 0)])


def local(projected, short_filters, decay_rate, residue, skip):
    tap_count = short_filters.shape[1]
    row_count = projected.shape[1]
    modes = decay_rate.shape[0]
    edge_rows = projected[:, row_count - (tap_count - 1) :, :]
    halo = from_behind(edge_rows, ("ctx", "dec"), 1)
    contribution = contributions(projected, halo, short_filters, decay_rate)
    received = lax.all_gather(contribution, "ctx", axis=0, tiled=False)
    shard_decay = jnp.exp(-decay_rate * row_count)
    chip_decay = shard_decay * shard_decay
    chip_here = lax.axis_index("ctx")
    running = jnp.zeros_like(contribution)
    entering = jnp.zeros_like(contribution)
    for chip in range(received.shape[0]):
        entering = jnp.where(chip_here == chip, running, entering)
        running = chip_decay * running + received[chip]
    core = lax.axis_index("dec")
    mine = jnp.concatenate([entering, running, contribution], axis=0)
    theirs = swap_cores(mine)
    first = jnp.where(core == 0, mine, theirs)
    second = jnp.where(core == 0, theirs, mine)
    chip_entering = shard_decay * first[:modes] + second[:modes]
    final_state = shard_decay * first[modes : 2 * modes] + second[modes : 2 * modes]
    prefix = jnp.where(core == 0, chip_entering, shard_decay * chip_entering + first[2 * modes :])
    mixed = mix(projected, halo, short_filters, decay_rate, residue, skip, prefix)
    return (mixed, final_state)


def solution(mesh):
    placed = (
        P(None, ("grp", "ctx", "dec"), "chan"),
        P(None, None, "chan"),
        P(None, "chan"),
        P(None, "chan"),
        P("chan"),
    )
    return jax.shard_map(
        local,
        mesh=mesh,
        in_specs=placed,
        out_specs=(P(("grp", "ctx", "dec"), "chan"), P("grp", "chan")),
        check_vma=False,
    )
```

```python
import functools

import jax
import jax.numpy as jnp
from jax import lax
from jax.experimental import pallas as pl
from jax.experimental.pallas import tpu as pltpu
from jax.sharding import PartitionSpec as P

CHAN_BLOCK = 512
ROW_GROUP = 8


def from_behind(value, axis, steps):
    count = lax.axis_size(axis)
    initial, last = (max(0, -steps), min(count, count - steps))
    return lax.ppermute(value, axis, [(source, source + steps) for source in range(initial, last)])


def _featurize_one(x_ref, halo_ref, filt_ref, index):
    x = x_ref[index].astype(jnp.float32)
    halo = halo_ref[index].astype(jnp.float32)
    taps = filt_ref[index]
    last = halo[halo.shape[0] - 1 : halo.shape[0]]
    second = halo[halo.shape[0] - 2 : halo.shape[0] - 1]
    body = taps[0:1] * x + taps[1:2] * pltpu.roll(x, 1, 0) + taps[2:3] * pltpu.roll(x, 2, 0)
    head_x = x[:ROW_GROUP]
    rows = lax.broadcasted_iota(jnp.int32, head_x.shape, 0)
    back1 = jnp.where(rows == 0, last, pltpu.roll(head_x, 1, 0))
    back2 = jnp.where(rows == 0, second, jnp.where(rows == 1, last, pltpu.roll(head_x, 2, 0)))
    head = taps[0:1] * head_x + taps[1:2] * back1 + taps[2:3] * back2
    return jnp.concatenate([head, body[ROW_GROUP:]], axis=0)


def _reduce_rows(ys):
    sub = lax.broadcasted_iota(jnp.int32, ys[0].shape, 0)
    low4 = sub < 4
    a = [jnp.where(low4, ys[i], ys[i + 4]) + pltpu.roll(jnp.where(low4, ys[i + 4], ys[i]), 4, 0) for i in range(4)]
    m2 = jnp.bitwise_and(sub, 3) < 2
    b = [jnp.where(m2, a[i] + pltpu.roll(a[i], 6, 0), a[i + 2] + pltpu.roll(a[i + 2], 2, 0)) for i in range(2)]
    m1 = jnp.bitwise_and(sub, 1) == 0
    return jnp.where(m1, b[0] + pltpu.roll(b[0], 7, 0), b[1] + pltpu.roll(b[1], 1, 0))


def _scan_rows(drive_ref, decay, residue, state, conv_ref):
    row_count = drive_ref.shape[0]
    low = slice(0, ROW_GROUP)
    high = slice(ROW_GROUP, 2 * ROW_GROUP)

    def body(group, state):
        start = pl.multiple_of(group * ROW_GROUP, ROW_GROUP)
        ys = []
        block = drive_ref[pl.ds(start, ROW_GROUP), :]
        for i in range(ROW_GROUP):
            drive_row = jnp.broadcast_to(block[i : i + 1], state.shape)
            state = decay * state + drive_row
            if conv_ref is not None:
                ys.append(residue[low] * state[low] + residue[high] * state[high])
        if conv_ref is not None:
            conv_ref[pl.ds(start, ROW_GROUP), :] = _reduce_rows(ys)
        return state

    return lax.fori_loop(0, row_count // ROW_GROUP, body, state)


def _contrib_kernel(x_ref, halo_ref, filt_ref, rate_ref, out_ref, drive_ref):
    k = _featurize_one(x_ref, halo_ref, filt_ref, 1)
    v = _featurize_one(x_ref, halo_ref, filt_ref, 2)
    drive_ref[...] = k * v
    decay = jnp.exp(-rate_ref[...])
    state = jnp.zeros(out_ref.shape, jnp.float32)
    out_ref[...] = _scan_rows(drive_ref, decay, None, state, None)


def _mix_kernel(x_ref, halo_ref, filt_ref, rate_ref, res_ref, skip_ref, init_ref, drive_ref, out_ref,
                conv_scr):
    decay = jnp.exp(-rate_ref[...])
    _scan_rows(drive_ref, decay, res_ref[...], init_ref[...], conv_scr)
    q = _featurize_one(x_ref, halo_ref, filt_ref, 0)
    out_ref[...] = (q * (conv_scr[...] + skip_ref[...] * drive_ref[...])).astype(out_ref.dtype)


def _specs(row_count, modes, taps, features=3):
    x_spec = pl.BlockSpec((features, row_count, CHAN_BLOCK), lambda j: (0, 0, j))
    halo_spec = pl.BlockSpec((features, taps - 1, CHAN_BLOCK), lambda j: (0, 0, j))
    filt_spec = pl.BlockSpec((features, taps, CHAN_BLOCK), lambda j: (0, 0, j))
    mode_spec = pl.BlockSpec((modes, CHAN_BLOCK), lambda j: (0, j))
    row_spec = pl.BlockSpec((1, CHAN_BLOCK), lambda j: (0, j))
    return x_spec, halo_spec, filt_spec, mode_spec, row_spec


def contributions(projected, halo, short_filters, decay_rate):
    _, row_count, chan_count = projected.shape
    modes = decay_rate.shape[0]
    taps = short_filters.shape[1]
    x_spec, halo_spec, filt_spec, mode_spec, _ = _specs(row_count, modes, taps)
    return pl.pallas_call(
        _contrib_kernel,
        grid=(chan_count // CHAN_BLOCK,),
        in_specs=[x_spec, halo_spec, filt_spec, mode_spec],
        out_specs=[mode_spec, pl.BlockSpec((row_count, CHAN_BLOCK), lambda j: (0, j))],
        out_shape=[
            jax.ShapeDtypeStruct((modes, chan_count), jnp.float32),
            jax.ShapeDtypeStruct((row_count, chan_count), jnp.float32),
        ],
    )(projected, halo, short_filters, decay_rate)


def mix(projected, halo, short_filters, decay_rate, residue, skip, prefix, drive):
    _, row_count, chan_count = projected.shape
    modes = decay_rate.shape[0]
    taps = short_filters.shape[1]
    x_spec, halo_spec, filt_spec, mode_spec, row_spec = _specs(row_count, modes, taps, 1)
    tile_spec = pl.BlockSpec((row_count, CHAN_BLOCK), lambda j: (0, j))
    return pl.pallas_call(
        _mix_kernel,
        grid=(chan_count // CHAN_BLOCK,),
        in_specs=[x_spec, halo_spec, filt_spec, mode_spec, mode_spec, row_spec, mode_spec, tile_spec],
        out_specs=tile_spec,
        out_shape=jax.ShapeDtypeStruct((row_count, chan_count), jnp.bfloat16),
        scratch_shapes=[pltpu.VMEM((row_count, CHAN_BLOCK), jnp.float32)],
    )(projected, halo, short_filters, decay_rate, residue, skip[None, :], prefix, drive)


def swap_cores(value):
    return lax.ppermute(value, "dec", [(0, 1), (1, 0)])


def local(projected, short_filters, decay_rate, residue, skip):
    tap_count = short_filters.shape[1]
    row_count = projected.shape[1]
    chan_count = projected.shape[2]
    edge_rows = projected[:, row_count - (tap_count - 1) :, :]
    halo = from_behind(edge_rows, ("ctx", "dec"), 1)
    contribution, drive = contributions(projected, halo, short_filters, decay_rate)
    core = lax.axis_index("dec")
    other = swap_cores(contribution)
    first_core = jnp.where(core == 0, contribution, other)
    second_core = jnp.where(core == 0, other, contribution)
    shard_decay = jnp.exp(-decay_rate * row_count)
    half = chan_count // 2
    start = core * half
    mine = lambda x: lax.dynamic_slice_in_dim(x, start, half, 1)
    chip_decay = mine(shard_decay) * mine(shard_decay)
    chip_part = mine(shard_decay) * mine(first_core) + mine(second_core)
    received = lax.all_gather(chip_part, "ctx", axis=0, tiled=False)
    chip_here = lax.axis_index("ctx")
    running = jnp.zeros_like(chip_part)
    entering = jnp.zeros_like(chip_part)
    for chip in range(received.shape[0]):
        entering = jnp.where(chip_here == chip, running, entering)
        running = chip_decay * running + received[chip]
    both = jnp.concatenate([entering, running], axis=0)
    other_both = swap_cores(both)
    low = jnp.where(core == 0, both, other_both)
    high = jnp.where(core == 0, other_both, both)
    whole = jnp.concatenate([low, high], axis=1)
    modes = decay_rate.shape[0]
    chip_entering = whole[:modes]
    final_state = whole[modes:]
    prefix = jnp.where(core == 0, chip_entering, shard_decay * chip_entering + first_core)
    mixed = mix(projected, halo, short_filters, decay_rate, residue, skip, prefix, drive)
    return (mixed, final_state)


def solution(mesh):
    placed = (
        P(None, ("grp", "ctx", "dec"), "chan"),
        P(None, None, "chan"),
        P(None, "chan"),
        P(None, "chan"),
        P("chan"),
    )
    return jax.shard_map(
        local,
        mesh=mesh,
        in_specs=placed,
        out_specs=(P(("grp", "ctx", "dec"), "chan"), P("grp", "chan")),
        check_vma=False,
    )
```

```python
import functools

import jax
import jax.numpy as jnp
from jax import lax
from jax.experimental import pallas as pl
from jax.experimental.pallas import tpu as pltpu
from jax.sharding import PartitionSpec as P

CHAN_BLOCK = 512
ROW_GROUP = 8


def from_behind(value, axis, steps):
    count = lax.axis_size(axis)
    initial, last = (max(0, -steps), min(count, count - steps))
    return lax.ppermute(value, axis, [(source, source + steps) for source in range(initial, last)])


def _featurize_one(x_ref, halo_ref, filt_ref, index):
    x = x_ref[index].astype(jnp.float32)
    halo = halo_ref[index].astype(jnp.float32)
    taps = filt_ref[index]
    last = halo[halo.shape[0] - 1 : halo.shape[0]]
    second = halo[halo.shape[0] - 2 : halo.shape[0] - 1]
    body = taps[0:1] * x + taps[1:2] * pltpu.roll(x, 1, 0) + taps[2:3] * pltpu.roll(x, 2, 0)
    head_x = x[:ROW_GROUP]
    rows = lax.broadcasted_iota(jnp.int32, head_x.shape, 0)
    back1 = jnp.where(rows == 0, last, pltpu.roll(head_x, 1, 0))
    back2 = jnp.where(rows == 0, second, jnp.where(rows == 1, last, pltpu.roll(head_x, 2, 0)))
    head = taps[0:1] * head_x + taps[1:2] * back1 + taps[2:3] * back2
    return jnp.concatenate([head, body[ROW_GROUP:]], axis=0)


def _reduce_rows(ys):
    sub = lax.broadcasted_iota(jnp.int32, ys[0].shape, 0)
    low4 = sub < 4
    a = [jnp.where(low4, ys[i], ys[i + 4]) + pltpu.roll(jnp.where(low4, ys[i + 4], ys[i]), 4, 0) for i in range(4)]
    m2 = jnp.bitwise_and(sub, 3) < 2
    b = [jnp.where(m2, a[i] + pltpu.roll(a[i], 6, 0), a[i + 2] + pltpu.roll(a[i + 2], 2, 0)) for i in range(2)]
    m1 = jnp.bitwise_and(sub, 1) == 0
    return jnp.where(m1, b[0] + pltpu.roll(b[0], 7, 0), b[1] + pltpu.roll(b[1], 1, 0))


def _scan_rows(drive_ref, decay, residue, state, conv_ref):
    row_count = drive_ref.shape[0]
    low = slice(0, ROW_GROUP)
    high = slice(ROW_GROUP, 2 * ROW_GROUP)

    def body(group, state):
        start = pl.multiple_of(group * ROW_GROUP, ROW_GROUP)
        ys = []
        block = drive_ref[pl.ds(start, ROW_GROUP), :]
        for i in range(ROW_GROUP):
            drive_row = jnp.broadcast_to(block[i : i + 1], state.shape)
            state = decay * state + drive_row
            if conv_ref is not None:
                ys.append(residue[low] * state[low] + residue[high] * state[high])
        if conv_ref is not None:
            conv_ref[pl.ds(start, ROW_GROUP), :] = _reduce_rows(ys)
        return state

    return lax.fori_loop(0, row_count // ROW_GROUP, body, state)


def _contrib_kernel(x_ref, halo_ref, filt_ref, rate_ref, out_ref, drive_ref):
    k = _featurize_one(x_ref, halo_ref, filt_ref, 1)
    v = _featurize_one(x_ref, halo_ref, filt_ref, 2)
    drive_ref[...] = k * v
    decay = jnp.exp(-rate_ref[...])
    state = jnp.zeros(out_ref.shape, jnp.float32)
    out_ref[...] = _scan_rows(drive_ref, decay, None, state, None)


def _mix_kernel(x_ref, halo_ref, filt_ref, rate_ref, res_ref, skip_ref, init_lo_ref, init_hi_ref,
                fin_lo_ref, fin_hi_ref, drive_ref, out_ref, fin_ref, conv_scr):
    in_low = pl.program_id(0) < pl.num_programs(0) // 2
    init = jnp.where(in_low, init_lo_ref[...], init_hi_ref[...])
    fin_ref[...] = jnp.where(in_low, fin_lo_ref[...], fin_hi_ref[...])
    decay = jnp.exp(-rate_ref[...])
    _scan_rows(drive_ref, decay, res_ref[...], init, conv_scr)
    q = _featurize_one(x_ref, halo_ref, filt_ref, 0)
    out_ref[...] = (q * (conv_scr[...] + skip_ref[...] * drive_ref[...])).astype(out_ref.dtype)


def _specs(row_count, modes, taps, features=3):
    x_spec = pl.BlockSpec((features, row_count, CHAN_BLOCK), lambda j: (0, 0, j))
    halo_spec = pl.BlockSpec((features, taps - 1, CHAN_BLOCK), lambda j: (0, 0, j))
    filt_spec = pl.BlockSpec((features, taps, CHAN_BLOCK), lambda j: (0, 0, j))
    mode_spec = pl.BlockSpec((modes, CHAN_BLOCK), lambda j: (0, j))
    row_spec = pl.BlockSpec((1, CHAN_BLOCK), lambda j: (0, j))
    return x_spec, halo_spec, filt_spec, mode_spec, row_spec


def contributions(projected, halo, short_filters, decay_rate):
    _, row_count, chan_count = projected.shape
    modes = decay_rate.shape[0]
    taps = short_filters.shape[1]
    x_spec, halo_spec, filt_spec, mode_spec, _ = _specs(row_count, modes, taps)
    return pl.pallas_call(
        _contrib_kernel,
        grid=(chan_count // CHAN_BLOCK,),
        in_specs=[x_spec, halo_spec, filt_spec, mode_spec],
        out_specs=[mode_spec, pl.BlockSpec((row_count, CHAN_BLOCK), lambda j: (0, j))],
        out_shape=[
            jax.ShapeDtypeStruct((modes, chan_count), jnp.float32),
            jax.ShapeDtypeStruct((row_count, chan_count), jnp.float32),
        ],
    )(projected, halo, short_filters, decay_rate)


def mix(projected, halo, short_filters, decay_rate, residue, skip, prefix_halves, final_halves, drive):
    _, row_count, chan_count = projected.shape
    modes = decay_rate.shape[0]
    taps = short_filters.shape[1]
    x_spec, halo_spec, filt_spec, mode_spec, row_spec = _specs(row_count, modes, taps, 1)
    tile_spec = pl.BlockSpec((row_count, CHAN_BLOCK), lambda j: (0, j))
    per_half = chan_count // 2 // CHAN_BLOCK
    low_spec = pl.BlockSpec((modes, CHAN_BLOCK), lambda j: (0, jnp.minimum(j, per_half - 1)))
    high_spec = pl.BlockSpec((modes, CHAN_BLOCK), lambda j: (0, jnp.maximum(j - per_half, 0)))
    return pl.pallas_call(
        _mix_kernel,
        grid=(chan_count // CHAN_BLOCK,),
        in_specs=[x_spec, halo_spec, filt_spec, mode_spec, mode_spec, row_spec,
                  low_spec, high_spec, low_spec, high_spec, tile_spec],
        out_specs=[tile_spec, mode_spec],
        out_shape=[
            jax.ShapeDtypeStruct((row_count, chan_count), jnp.bfloat16),
            jax.ShapeDtypeStruct((modes, chan_count), jnp.float32),
        ],
        scratch_shapes=[pltpu.VMEM((row_count, CHAN_BLOCK), jnp.float32)],
    )(projected, halo, short_filters, decay_rate, residue, skip[None, :], *prefix_halves,
      *final_halves, drive)


def swap_cores(value):
    return lax.ppermute(value, "dec", [(0, 1), (1, 0)])


def local(projected, short_filters, decay_rate, residue, skip):
    tap_count = short_filters.shape[1]
    row_count = projected.shape[1]
    chan_count = projected.shape[2]
    modes = decay_rate.shape[0]
    edge_rows = projected[:, row_count - (tap_count - 1) :, :]
    halo = from_behind(edge_rows, ("ctx", "dec"), 1)
    contribution, drive = contributions(projected, halo, short_filters, decay_rate)
    core = lax.axis_index("dec")
    first = core == 0
    half = chan_count // 2
    pick = lambda x: jnp.where(first, x[:, :half], x[:, half:])
    other_half = lambda x: jnp.where(first, x[:, half:], x[:, :half])
    kept = pick(contribution)
    partner = swap_cores(other_half(contribution))
    shard_decay = pick(jnp.exp(-decay_rate * row_count))
    first_core = jnp.where(first, kept, partner)
    second_core = jnp.where(first, partner, kept)
    chip_part = shard_decay * first_core + second_core
    received = lax.all_gather(chip_part, "ctx", axis=0, tiled=False)
    chip_here = lax.axis_index("ctx")
    chip_decay = shard_decay * shard_decay
    running = jnp.zeros_like(chip_part)
    entering = jnp.zeros_like(chip_part)
    for chip in range(received.shape[0]):
        entering = jnp.where(chip_here == chip, running, entering)
        running = chip_decay * running + received[chip]
    second_entering = shard_decay * entering + first_core
    both = jnp.concatenate([entering, running, second_entering], axis=0)
    other_both = swap_cores(both)
    low = jnp.where(first, both, other_both)
    high = jnp.where(first, other_both, both)
    prefix_halves = (
        jnp.where(first, low[:modes], low[2 * modes :]),
        jnp.where(first, high[:modes], high[2 * modes :]),
    )
    final_halves = (low[modes : 2 * modes], high[modes : 2 * modes])
    mixed, final_state = mix(projected, halo, short_filters, decay_rate, residue, skip,
                             prefix_halves, final_halves, drive)
    return (mixed, final_state)


def solution(mesh):
    placed = (
        P(None, ("grp", "ctx", "dec"), "chan"),
        P(None, None, "chan"),
        P(None, "chan"),
        P(None, "chan"),
        P("chan"),
    )
    return jax.shard_map(
        local,
        mesh=mesh,
        in_specs=placed,
        out_specs=(P(("grp", "ctx", "dec"), "chan"), P("grp", "chan")),
        check_vma=False,
    )
```

```python
import functools

import jax
import jax.numpy as jnp
from jax import lax
from jax.experimental import pallas as pl
from jax.experimental.pallas import tpu as pltpu
from jax.sharding import PartitionSpec as P

CHAN_BLOCK = 1024
LANE_BLOCK = 512
ROW_GROUP = 8


def from_behind(value, axis, steps):
    count = lax.axis_size(axis)
    initial, last = (max(0, -steps), min(count, count - steps))
    return lax.ppermute(value, axis, [(source, source + steps) for source in range(initial, last)])


def _featurize_one(x_ref, halo_ref, filt_ref, index):
    x = x_ref[index].astype(jnp.float32)
    halo = halo_ref[index].astype(jnp.float32)
    taps = filt_ref[index]
    last = halo[halo.shape[0] - 1 : halo.shape[0]]
    second = halo[halo.shape[0] - 2 : halo.shape[0] - 1]
    body = taps[0:1] * x + taps[1:2] * pltpu.roll(x, 1, 0) + taps[2:3] * pltpu.roll(x, 2, 0)
    head_x = x[:ROW_GROUP]
    rows = lax.broadcasted_iota(jnp.int32, head_x.shape, 0)
    back1 = jnp.where(rows == 0, last, pltpu.roll(head_x, 1, 0))
    back2 = jnp.where(rows == 0, second, jnp.where(rows == 1, last, pltpu.roll(head_x, 2, 0)))
    head = taps[0:1] * head_x + taps[1:2] * back1 + taps[2:3] * back2
    return jnp.concatenate([head, body[ROW_GROUP:]], axis=0)


def _reduce_rows(ys):
    sub = lax.broadcasted_iota(jnp.int32, ys[0].shape, 0)
    low4 = sub < 4
    a = [jnp.where(low4, ys[i], ys[i + 4]) + pltpu.roll(jnp.where(low4, ys[i + 4], ys[i]), 4, 0) for i in range(4)]
    m2 = jnp.bitwise_and(sub, 3) < 2
    b = [jnp.where(m2, a[i] + pltpu.roll(a[i], 6, 0), a[i + 2] + pltpu.roll(a[i + 2], 2, 0)) for i in range(2)]
    m1 = jnp.bitwise_and(sub, 1) == 0
    return jnp.where(m1, b[0] + pltpu.roll(b[0], 7, 0), b[1] + pltpu.roll(b[1], 1, 0))


def _scan_rows(drive_ref, decay, residue, state, conv_ref):
    row_count = drive_ref.shape[0]
    low = slice(0, ROW_GROUP)
    high = slice(ROW_GROUP, 2 * ROW_GROUP)
    finals = []
    for lane_start in range(0, drive_ref.shape[1], LANE_BLOCK):
        lanes = slice(lane_start, lane_start + LANE_BLOCK)
        decay_part = decay[:, lanes]
        residue_part = None if residue is None else residue[:, lanes]

        def body(group, state):
            start = pl.multiple_of(group * ROW_GROUP, ROW_GROUP)
            ys = []
            block = drive_ref[pl.ds(start, ROW_GROUP), lanes]
            for i in range(ROW_GROUP):
                drive_row = jnp.broadcast_to(block[i : i + 1], state.shape)
                state = decay_part * state + drive_row
                if conv_ref is not None:
                    ys.append(residue_part[low] * state[low] + residue_part[high] * state[high])
            if conv_ref is not None:
                conv_ref[pl.ds(start, ROW_GROUP), lanes] = _reduce_rows(ys)
            return state

        finals.append(lax.fori_loop(0, row_count // ROW_GROUP, body, state[:, lanes]))
    return jnp.concatenate(finals, axis=1)


def _contrib_kernel(x_ref, halo_ref, filt_ref, rate_ref, out_ref, drive_ref):
    k = _featurize_one(x_ref, halo_ref, filt_ref, 1)
    v = _featurize_one(x_ref, halo_ref, filt_ref, 2)
    drive_ref[...] = k * v
    decay = jnp.exp(-rate_ref[...])
    state = jnp.zeros(out_ref.shape, jnp.float32)
    out_ref[...] = _scan_rows(drive_ref, decay, None, state, None)


def _mix_kernel(x_ref, halo_ref, filt_ref, rate_ref, res_ref, skip_ref, init_ref, drive_ref, out_ref,
                conv_scr):
    decay = jnp.exp(-rate_ref[...])
    _scan_rows(drive_ref, decay, res_ref[...], init_ref[...], conv_scr)
    q = _featurize_one(x_ref, halo_ref, filt_ref, 0)
    out_ref[...] = (q * (conv_scr[...] + skip_ref[...] * drive_ref[...])).astype(out_ref.dtype)


def _specs(row_count, modes, taps, features=3):
    x_spec = pl.BlockSpec((features, row_count, CHAN_BLOCK), lambda j: (0, 0, j))
    halo_spec = pl.BlockSpec((features, taps - 1, CHAN_BLOCK), lambda j: (0, 0, j))
    filt_spec = pl.BlockSpec((features, taps, CHAN_BLOCK), lambda j: (0, 0, j))
    mode_spec = pl.BlockSpec((modes, CHAN_BLOCK), lambda j: (0, j))
    row_spec = pl.BlockSpec((1, CHAN_BLOCK), lambda j: (0, j))
    return x_spec, halo_spec, filt_spec, mode_spec, row_spec


def contributions(projected, halo, short_filters, decay_rate):
    _, row_count, chan_count = projected.shape
    modes = decay_rate.shape[0]
    taps = short_filters.shape[1]
    x_spec, halo_spec, filt_spec, mode_spec, _ = _specs(row_count, modes, taps)
    return pl.pallas_call(
        _contrib_kernel,
        grid=(chan_count // CHAN_BLOCK,),
        in_specs=[x_spec, halo_spec, filt_spec, mode_spec],
        out_specs=[mode_spec, pl.BlockSpec((row_count, CHAN_BLOCK), lambda j: (0, j))],
        out_shape=[
            jax.ShapeDtypeStruct((modes, chan_count), jnp.float32),
            jax.ShapeDtypeStruct((row_count, chan_count), jnp.float32),
        ],
    )(projected, halo, short_filters, decay_rate)


def mix(projected, halo, short_filters, decay_rate, residue, skip, prefix, drive):
    _, row_count, chan_count = projected.shape
    modes = decay_rate.shape[0]
    taps = short_filters.shape[1]
    x_spec, halo_spec, filt_spec, mode_spec, row_spec = _specs(row_count, modes, taps, 1)
    tile_spec = pl.BlockSpec((row_count, CHAN_BLOCK), lambda j: (0, j))
    return pl.pallas_call(
        _mix_kernel,
        grid=(chan_count // CHAN_BLOCK,),
        in_specs=[x_spec, halo_spec, filt_spec, mode_spec, mode_spec, row_spec, mode_spec, tile_spec],
        out_specs=tile_spec,
        out_shape=jax.ShapeDtypeStruct((row_count, chan_count), jnp.bfloat16),
        scratch_shapes=[pltpu.VMEM((row_count, CHAN_BLOCK), jnp.float32)],
    )(projected, halo, short_filters, decay_rate, residue, skip[None, :], prefix, drive)


def swap_cores(value):
    return lax.ppermute(value, "dec", [(0, 1), (1, 0)])


def local(projected, short_filters, decay_rate, residue, skip):
    tap_count = short_filters.shape[1]
    row_count = projected.shape[1]
    chan_count = projected.shape[2]
    edge_rows = projected[:, row_count - (tap_count - 1) :, :]
    halo = from_behind(edge_rows, ("ctx", "dec"), 1)
    contribution, drive = contributions(projected, halo, short_filters, decay_rate)
    core = lax.axis_index("dec")
    other = swap_cores(contribution)
    first_core = jnp.where(core == 0, contribution, other)
    second_core = jnp.where(core == 0, other, contribution)
    shard_decay = jnp.exp(-decay_rate * row_count)
    half = chan_count // 2
    start = core * half
    mine = lambda x: lax.dynamic_slice_in_dim(x, start, half, 1)
    chip_decay = mine(shard_decay) * mine(shard_decay)
    chip_part = mine(shard_decay) * mine(first_core) + mine(second_core)
    received = lax.all_gather(chip_part, "ctx", axis=0, tiled=False)
    chip_here = lax.axis_index("ctx")
    running = jnp.zeros_like(chip_part)
    entering = jnp.zeros_like(chip_part)
    for chip in range(received.shape[0]):
        entering = jnp.where(chip_here == chip, running, entering)
        running = chip_decay * running + received[chip]
    both = jnp.concatenate([entering, running], axis=0)
    other_both = swap_cores(both)
    low = jnp.where(core == 0, both, other_both)
    high = jnp.where(core == 0, other_both, both)
    whole = jnp.concatenate([low, high], axis=1)
    modes = decay_rate.shape[0]
    chip_entering = whole[:modes]
    final_state = whole[modes:]
    prefix = jnp.where(core == 0, chip_entering, shard_decay * chip_entering + first_core)
    mixed = mix(projected, halo, short_filters, decay_rate, residue, skip, prefix, drive)
    return (mixed, final_state)


def solution(mesh):
    placed = (
        P(None, ("grp", "ctx", "dec"), "chan"),
        P(None, None, "chan"),
        P(None, "chan"),
        P(None, "chan"),
        P("chan"),
    )
    return jax.shard_map(
        local,
        mesh=mesh,
        in_specs=placed,
        out_specs=(P(("grp", "ctx", "dec"), "chan"), P("grp", "chan")),
        check_vma=False,
    )
```

```python
import functools

import jax
import jax.numpy as jnp
from jax import lax
from jax.experimental import pallas as pl
from jax.experimental.pallas import tpu as pltpu
from jax.sharding import PartitionSpec as P

CHAN_BLOCK = 1024
CONTRIB_BLOCK = 2048
LANE_BLOCK = 512
ROW_GROUP = 8


def from_behind(value, axis, steps):
    count = lax.axis_size(axis)
    initial, last = (max(0, -steps), min(count, count - steps))
    return lax.ppermute(value, axis, [(source, source + steps) for source in range(initial, last)])


def _featurize_one(x_ref, halo_ref, filt_ref, index):
    x = x_ref[index].astype(jnp.float32)
    halo = halo_ref[index].astype(jnp.float32)
    taps = filt_ref[index]
    last = halo[halo.shape[0] - 1 : halo.shape[0]]
    second = halo[halo.shape[0] - 2 : halo.shape[0] - 1]
    body = taps[0:1] * x + taps[1:2] * pltpu.roll(x, 1, 0) + taps[2:3] * pltpu.roll(x, 2, 0)
    head_x = x[:ROW_GROUP]
    rows = lax.broadcasted_iota(jnp.int32, head_x.shape, 0)
    back1 = jnp.where(rows == 0, last, pltpu.roll(head_x, 1, 0))
    back2 = jnp.where(rows == 0, second, jnp.where(rows == 1, last, pltpu.roll(head_x, 2, 0)))
    head = taps[0:1] * head_x + taps[1:2] * back1 + taps[2:3] * back2
    return jnp.concatenate([head, body[ROW_GROUP:]], axis=0)


def _reduce_rows(ys):
    sub = lax.broadcasted_iota(jnp.int32, ys[0].shape, 0)
    low4 = sub < 4
    a = [jnp.where(low4, ys[i], ys[i + 4]) + pltpu.roll(jnp.where(low4, ys[i + 4], ys[i]), 4, 0) for i in range(4)]
    m2 = jnp.bitwise_and(sub, 3) < 2
    b = [jnp.where(m2, a[i] + pltpu.roll(a[i], 6, 0), a[i + 2] + pltpu.roll(a[i + 2], 2, 0)) for i in range(2)]
    m1 = jnp.bitwise_and(sub, 1) == 0
    return jnp.where(m1, b[0] + pltpu.roll(b[0], 7, 0), b[1] + pltpu.roll(b[1], 1, 0))


def _scan_rows(drive_ref, decay, residue, state, conv_ref):
    row_count = drive_ref.shape[0]
    low = slice(0, ROW_GROUP)
    high = slice(ROW_GROUP, 2 * ROW_GROUP)
    finals = []
    for lane_start in range(0, drive_ref.shape[1], LANE_BLOCK):
        lanes = slice(lane_start, lane_start + LANE_BLOCK)
        decay_part = decay[:, lanes]
        residue_part = None if residue is None else residue[:, lanes]

        def body(group, state):
            start = pl.multiple_of(group * ROW_GROUP, ROW_GROUP)
            ys = []
            block = drive_ref[pl.ds(start, ROW_GROUP), lanes]
            for i in range(ROW_GROUP):
                drive_row = jnp.broadcast_to(block[i : i + 1], state.shape)
                state = decay_part * state + drive_row
                if conv_ref is not None:
                    ys.append(residue_part[low] * state[low] + residue_part[high] * state[high])
            if conv_ref is not None:
                conv_ref[pl.ds(start, ROW_GROUP), lanes] = _reduce_rows(ys)
            return state

        finals.append(lax.fori_loop(0, row_count // ROW_GROUP, body, state[:, lanes]))
    return jnp.concatenate(finals, axis=1)


def _contrib_kernel(x_ref, halo_ref, filt_ref, rate_ref, out_ref, drive_ref):
    k = _featurize_one(x_ref, halo_ref, filt_ref, 1)
    v = _featurize_one(x_ref, halo_ref, filt_ref, 2)
    drive_ref[...] = k * v
    decay = jnp.exp(-rate_ref[...])
    state = jnp.zeros(out_ref.shape, jnp.float32)
    out_ref[...] = _scan_rows(drive_ref, decay, None, state, None)


def _mix_kernel(x_ref, halo_ref, filt_ref, rate_ref, res_ref, skip_ref, init_ref, drive_ref, out_ref,
                conv_scr):
    decay = jnp.exp(-rate_ref[...])
    _scan_rows(drive_ref, decay, res_ref[...], init_ref[...], conv_scr)
    q = _featurize_one(x_ref, halo_ref, filt_ref, 0)
    out_ref[...] = (q * (conv_scr[...] + skip_ref[...] * drive_ref[...])).astype(out_ref.dtype)


def _specs(row_count, modes, taps, features=3, block=CHAN_BLOCK):
    x_spec = pl.BlockSpec((features, row_count, block), lambda j: (0, 0, j))
    halo_spec = pl.BlockSpec((features, taps - 1, block), lambda j: (0, 0, j))
    filt_spec = pl.BlockSpec((features, taps, block), lambda j: (0, 0, j))
    mode_spec = pl.BlockSpec((modes, block), lambda j: (0, j))
    row_spec = pl.BlockSpec((1, block), lambda j: (0, j))
    return x_spec, halo_spec, filt_spec, mode_spec, row_spec


def contributions(projected, halo, short_filters, decay_rate):
    _, row_count, chan_count = projected.shape
    modes = decay_rate.shape[0]
    taps = short_filters.shape[1]
    block = min(CONTRIB_BLOCK, chan_count)
    x_spec, halo_spec, filt_spec, mode_spec, _ = _specs(row_count, modes, taps, 3, block)
    return pl.pallas_call(
        _contrib_kernel,
        grid=(chan_count // block,),
        in_specs=[x_spec, halo_spec, filt_spec, mode_spec],
        out_specs=[mode_spec, pl.BlockSpec((row_count, block), lambda j: (0, j))],
        out_shape=[
            jax.ShapeDtypeStruct((modes, chan_count), jnp.float32),
            jax.ShapeDtypeStruct((row_count, chan_count), jnp.float32),
        ],
    )(projected, halo, short_filters, decay_rate)


def mix(projected, halo, short_filters, decay_rate, residue, skip, prefix, drive):
    _, row_count, chan_count = projected.shape
    modes = decay_rate.shape[0]
    taps = short_filters.shape[1]
    block = min(CHAN_BLOCK, chan_count)
    x_spec, halo_spec, filt_spec, mode_spec, row_spec = _specs(row_count, modes, taps, 1, block)
    tile_spec = pl.BlockSpec((row_count, block), lambda j: (0, j))
    return pl.pallas_call(
        _mix_kernel,
        grid=(chan_count // block,),
        in_specs=[x_spec, halo_spec, filt_spec, mode_spec, mode_spec, row_spec, mode_spec, tile_spec],
        out_specs=tile_spec,
        out_shape=jax.ShapeDtypeStruct((row_count, chan_count), jnp.bfloat16),
        scratch_shapes=[pltpu.VMEM((row_count, block), jnp.float32)],
    )(projected, halo, short_filters, decay_rate, residue, skip[None, :], prefix, drive)


def swap_cores(value):
    return lax.ppermute(value, "dec", [(0, 1), (1, 0)])


def local(projected, short_filters, decay_rate, residue, skip):
    tap_count = short_filters.shape[1]
    row_count = projected.shape[1]
    chan_count = projected.shape[2]
    edge_rows = projected[:, row_count - (tap_count - 1) :, :]
    halo = from_behind(edge_rows, ("ctx", "dec"), 1)
    contribution, drive = contributions(projected, halo, short_filters, decay_rate)
    core = lax.axis_index("dec")
    other = swap_cores(contribution)
    first_core = jnp.where(core == 0, contribution, other)
    second_core = jnp.where(core == 0, other, contribution)
    shard_decay = jnp.exp(-decay_rate * row_count)
    half = chan_count // 2
    start = core * half
    mine = lambda x: lax.dynamic_slice_in_dim(x, start, half, 1)
    chip_decay = mine(shard_decay) * mine(shard_decay)
    chip_part = mine(shard_decay) * mine(first_core) + mine(second_core)
    received = lax.all_gather(chip_part, "ctx", axis=0, tiled=False)
    chip_here = lax.axis_index("ctx")
    running = jnp.zeros_like(chip_part)
    entering = jnp.zeros_like(chip_part)
    for chip in range(received.shape[0]):
        entering = jnp.where(chip_here == chip, running, entering)
        running = chip_decay * running + received[chip]
    both = jnp.concatenate([entering, running], axis=0)
    other_both = swap_cores(both)
    low = jnp.where(core == 0, both, other_both)
    high = jnp.where(core == 0, other_both, both)
    whole = jnp.concatenate([low, high], axis=1)
    modes = decay_rate.shape[0]
    chip_entering = whole[:modes]
    final_state = whole[modes:]
    prefix = jnp.where(core == 0, chip_entering, shard_decay * chip_entering + first_core)
    mixed = mix(projected, halo, short_filters, decay_rate, residue, skip, prefix, drive)
    return (mixed, final_state)


def solution(mesh):
    placed = (
        P(None, ("grp", "ctx", "dec"), "chan"),
        P(None, None, "chan"),
        P(None, "chan"),
        P(None, "chan"),
        P("chan"),
    )
    return jax.shard_map(
        local,
        mesh=mesh,
        in_specs=placed,
        out_specs=(P(("grp", "ctx", "dec"), "chan"), P("grp", "chan")),
        check_vma=False,
    )
```

```python
import functools

import jax
import jax.numpy as jnp
from jax import lax
from jax.experimental import pallas as pl
from jax.experimental.pallas import tpu as pltpu
from jax.sharding import PartitionSpec as P

CHAN_BLOCK = 1024
LANE_BLOCK = 512
ROW_GROUP = 8


def from_behind(value, axis, steps):
    count = lax.axis_size(axis)
    initial, last = (max(0, -steps), min(count, count - steps))
    return lax.ppermute(value, axis, [(source, source + steps) for source in range(initial, last)])


def _featurize_one(x_ref, halo_ref, filt_ref, index):
    x = x_ref[index].astype(jnp.float32)
    halo = halo_ref[index].astype(jnp.float32)
    taps = filt_ref[index]
    last = halo[halo.shape[0] - 1 : halo.shape[0]]
    second = halo[halo.shape[0] - 2 : halo.shape[0] - 1]
    body = taps[0:1] * x + taps[1:2] * pltpu.roll(x, 1, 0) + taps[2:3] * pltpu.roll(x, 2, 0)
    head_x = x[:ROW_GROUP]
    rows = lax.broadcasted_iota(jnp.int32, head_x.shape, 0)
    back1 = jnp.where(rows == 0, last, pltpu.roll(head_x, 1, 0))
    back2 = jnp.where(rows == 0, second, jnp.where(rows == 1, last, pltpu.roll(head_x, 2, 0)))
    head = taps[0:1] * head_x + taps[1:2] * back1 + taps[2:3] * back2
    return jnp.concatenate([head, body[ROW_GROUP:]], axis=0)


def _reduce_rows(ys):
    sub = lax.broadcasted_iota(jnp.int32, ys[0].shape, 0)
    low4 = sub < 4
    a = [jnp.where(low4, ys[i], ys[i + 4]) + pltpu.roll(jnp.where(low4, ys[i + 4], ys[i]), 4, 0) for i in range(4)]
    m2 = jnp.bitwise_and(sub, 3) < 2
    b = [jnp.where(m2, a[i] + pltpu.roll(a[i], 6, 0), a[i + 2] + pltpu.roll(a[i + 2], 2, 0)) for i in range(2)]
    m1 = jnp.bitwise_and(sub, 1) == 0
    return jnp.where(m1, b[0] + pltpu.roll(b[0], 7, 0), b[1] + pltpu.roll(b[1], 1, 0))


def _scan_rows(drive_ref, decay, residue, state, conv_ref):
    row_count = drive_ref.shape[0]
    low = slice(0, ROW_GROUP)
    high = slice(ROW_GROUP, 2 * ROW_GROUP)
    finals = []
    for lane_start in range(0, drive_ref.shape[1], LANE_BLOCK):
        lanes = slice(lane_start, lane_start + LANE_BLOCK)
        decay_part = decay[:, lanes]
        residue_part = None if residue is None else residue[:, lanes]

        def body(group, state):
            start = pl.multiple_of(group * ROW_GROUP, ROW_GROUP)
            ys = []
            block = drive_ref[pl.ds(start, ROW_GROUP), lanes]
            for i in range(ROW_GROUP):
                drive_row = jnp.broadcast_to(block[i : i + 1], state.shape)
                state = decay_part * state + drive_row
                if conv_ref is not None:
                    ys.append(residue_part[low] * state[low] + residue_part[high] * state[high])
            if conv_ref is not None:
                conv_ref[pl.ds(start, ROW_GROUP), lanes] = _reduce_rows(ys)
            return state

        finals.append(lax.fori_loop(0, row_count // ROW_GROUP, body, state[:, lanes]))
    return jnp.concatenate(finals, axis=1)


def _contrib_kernel(x_ref, halo_ref, filt_ref, rate_ref, out_ref, drive_ref):
    k = _featurize_one(x_ref, halo_ref, filt_ref, 1)
    v = _featurize_one(x_ref, halo_ref, filt_ref, 2)
    drive_ref[...] = k * v
    decay = jnp.exp(-rate_ref[...])
    block = rate_ref.shape[1]
    start = pl.multiple_of(pl.program_id(0) * block, block)
    state = jnp.zeros(rate_ref.shape, jnp.float32)
    out_ref[:, pl.ds(start, block)] = _scan_rows(drive_ref, decay, None, state, None)


def _mix_kernel(x_ref, halo_ref, filt_ref, rate_ref, res_ref, skip_ref, init_ref, fin_in_ref, drive_ref,
                out_ref, fin_ref, conv_scr):
    block = rate_ref.shape[1]
    start = pl.multiple_of(pl.program_id(0) * block, block)
    fin_ref[...] = fin_in_ref[:, pl.ds(start, block)]
    decay = jnp.exp(-rate_ref[...])
    _scan_rows(drive_ref, decay, res_ref[...], init_ref[:, pl.ds(start, block)], conv_scr)
    q = _featurize_one(x_ref, halo_ref, filt_ref, 0)
    out_ref[...] = (q * (conv_scr[...] + skip_ref[...] * drive_ref[...])).astype(out_ref.dtype)


def _specs(row_count, modes, taps, features=3):
    x_spec = pl.BlockSpec((features, row_count, CHAN_BLOCK), lambda j: (0, 0, j))
    halo_spec = pl.BlockSpec((features, taps - 1, CHAN_BLOCK), lambda j: (0, 0, j))
    filt_spec = pl.BlockSpec((features, taps, CHAN_BLOCK), lambda j: (0, 0, j))
    mode_spec = pl.BlockSpec((modes, CHAN_BLOCK), lambda j: (0, j))
    row_spec = pl.BlockSpec((1, CHAN_BLOCK), lambda j: (0, j))
    return x_spec, halo_spec, filt_spec, mode_spec, row_spec


def contributions(projected, halo, short_filters, decay_rate):
    _, row_count, chan_count = projected.shape
    modes = decay_rate.shape[0]
    taps = short_filters.shape[1]
    x_spec, halo_spec, filt_spec, mode_spec, _ = _specs(row_count, modes, taps)
    return pl.pallas_call(
        _contrib_kernel,
        grid=(chan_count // CHAN_BLOCK,),
        in_specs=[x_spec, halo_spec, filt_spec, mode_spec],
        out_specs=[pl.BlockSpec(memory_space=pltpu.VMEM), pl.BlockSpec((row_count, CHAN_BLOCK), lambda j: (0, j))],
        out_shape=[
            jax.ShapeDtypeStruct((modes, chan_count), jnp.float32),
            jax.ShapeDtypeStruct((row_count, chan_count), jnp.float32),
        ],
    )(projected, halo, short_filters, decay_rate)


def mix(projected, halo, short_filters, decay_rate, residue, skip, prefix, final_state, drive):
    _, row_count, chan_count = projected.shape
    modes = decay_rate.shape[0]
    taps = short_filters.shape[1]
    x_spec, halo_spec, filt_spec, mode_spec, row_spec = _specs(row_count, modes, taps, 1)
    tile_spec = pl.BlockSpec((row_count, CHAN_BLOCK), lambda j: (0, j))
    whole = pl.BlockSpec(memory_space=pltpu.VMEM)
    return pl.pallas_call(
        _mix_kernel,
        grid=(chan_count // CHAN_BLOCK,),
        in_specs=[x_spec, halo_spec, filt_spec, mode_spec, mode_spec, row_spec, whole, whole, tile_spec],
        out_specs=[tile_spec, mode_spec],
        out_shape=[
            jax.ShapeDtypeStruct((row_count, chan_count), jnp.bfloat16),
            jax.ShapeDtypeStruct((modes, chan_count), jnp.float32),
        ],
        scratch_shapes=[pltpu.VMEM((row_count, CHAN_BLOCK), jnp.float32)],
    )(projected, halo, short_filters, decay_rate, residue, skip[None, :], prefix, final_state, drive)


def swap_cores(value):
    return lax.ppermute(value, "dec", [(0, 1), (1, 0)])


def local(projected, short_filters, decay_rate, residue, skip):
    tap_count = short_filters.shape[1]
    row_count = projected.shape[1]
    chan_count = projected.shape[2]
    modes = decay_rate.shape[0]
    edge_rows = projected[:, row_count - (tap_count - 1) :, :]
    halo = from_behind(edge_rows, ("ctx", "dec"), 1)
    contribution, drive = contributions(projected, halo, short_filters, decay_rate)
    core = lax.axis_index("dec")
    first = core == 0
    other = swap_cores(contribution)
    shard_decay = jnp.exp(-decay_rate * row_count)
    half = chan_count // 2
    lo = lambda x: x[:, :half]
    hi = lambda x: x[:, half:]
    chip_part = jnp.where(
        first,
        lo(shard_decay) * lo(contribution) + lo(other),
        hi(shard_decay) * hi(other) + hi(contribution),
    )
    half_decay = jnp.where(first, lo(shard_decay), hi(shard_decay))
    received = lax.all_gather(chip_part, "ctx", axis=0, tiled=False)
    chip_here = lax.axis_index("ctx")
    chip_decay = half_decay * half_decay
    running = jnp.zeros_like(chip_part)
    entering = jnp.zeros_like(chip_part)
    for chip in range(received.shape[0]):
        entering = jnp.where(chip_here == chip, running, entering)
        running = chip_decay * running + received[chip]
    both = jnp.concatenate([entering, running], axis=0)
    other_both = swap_cores(both)
    low = jnp.where(first, both, other_both)
    high = jnp.where(first, other_both, both)
    whole = jnp.concatenate([low, high], axis=1)
    chip_entering = whole[:modes]
    final_state = whole[modes:]
    prefix = jnp.where(first, chip_entering, shard_decay * chip_entering + other)
    mixed, final_state = mix(projected, halo, short_filters, decay_rate, residue, skip, prefix,
                             final_state, drive)
    return (mixed, final_state)


def solution(mesh):
    placed = (
        P(None, ("grp", "ctx", "dec"), "chan"),
        P(None, None, "chan"),
        P(None, "chan"),
        P(None, "chan"),
        P("chan"),
    )
    return jax.shard_map(
        local,
        mesh=mesh,
        in_specs=placed,
        out_specs=(P(("grp", "ctx", "dec"), "chan"), P("grp", "chan")),
        check_vma=False,
    )
```

```python
import functools

import jax
import jax.numpy as jnp
from jax import lax
from jax.experimental import pallas as pl
from jax.experimental.pallas import tpu as pltpu
from jax.sharding import PartitionSpec as P

CHAN_BLOCK = 1024
LANE_BLOCK = 512
ROW_GROUP = 8


def from_behind(value, axis, steps):
    count = lax.axis_size(axis)
    initial, last = (max(0, -steps), min(count, count - steps))
    return lax.ppermute(value, axis, [(source, source + steps) for source in range(initial, last)])


def _featurize_one(x_ref, halo_ref, filt_ref, index):
    x = x_ref[index].astype(jnp.float32)
    halo = halo_ref[index].astype(jnp.float32)
    taps = filt_ref[index]
    last = halo[halo.shape[0] - 1 : halo.shape[0]]
    second = halo[halo.shape[0] - 2 : halo.shape[0] - 1]
    body = taps[0:1] * x + taps[1:2] * pltpu.roll(x, 1, 0) + taps[2:3] * pltpu.roll(x, 2, 0)
    head_x = x[:ROW_GROUP]
    rows = lax.broadcasted_iota(jnp.int32, head_x.shape, 0)
    back1 = jnp.where(rows == 0, last, pltpu.roll(head_x, 1, 0))
    back2 = jnp.where(rows == 0, second, jnp.where(rows == 1, last, pltpu.roll(head_x, 2, 0)))
    head = taps[0:1] * head_x + taps[1:2] * back1 + taps[2:3] * back2
    return jnp.concatenate([head, body[ROW_GROUP:]], axis=0)


def _reduce_rows(ys):
    sub = lax.broadcasted_iota(jnp.int32, ys[0].shape, 0)
    low4 = sub < 4
    a = [jnp.where(low4, ys[i], ys[i + 4]) + pltpu.roll(jnp.where(low4, ys[i + 4], ys[i]), 4, 0) for i in range(4)]
    m2 = jnp.bitwise_and(sub, 3) < 2
    b = [jnp.where(m2, a[i] + pltpu.roll(a[i], 6, 0), a[i + 2] + pltpu.roll(a[i + 2], 2, 0)) for i in range(2)]
    m1 = jnp.bitwise_and(sub, 1) == 0
    return jnp.where(m1, b[0] + pltpu.roll(b[0], 7, 0), b[1] + pltpu.roll(b[1], 1, 0))


def _scan_rows(drive_ref, decay, residue, state, conv_ref):
    row_count = drive_ref.shape[0]
    low = slice(0, ROW_GROUP)
    high = slice(ROW_GROUP, 2 * ROW_GROUP)
    finals = []
    for lane_start in range(0, drive_ref.shape[1], LANE_BLOCK):
        lanes = slice(lane_start, lane_start + LANE_BLOCK)
        decay_part = decay[:, lanes]
        residue_part = None if residue is None else residue[:, lanes]

        def body(group, state):
            start = pl.multiple_of(group * ROW_GROUP, ROW_GROUP)
            ys = []
            block = drive_ref[pl.ds(start, ROW_GROUP), lanes]
            for i in range(ROW_GROUP):
                drive_row = jnp.broadcast_to(block[i : i + 1], state.shape)
                state = decay_part * state + drive_row
                if conv_ref is not None:
                    ys.append(residue_part[low] * state[low] + residue_part[high] * state[high])
            if conv_ref is not None:
                conv_ref[pl.ds(start, ROW_GROUP), lanes] = _reduce_rows(ys)
            return state

        finals.append(lax.fori_loop(0, row_count // ROW_GROUP, body, state[:, lanes]))
    return jnp.concatenate(finals, axis=1)


def _contrib_kernel(x_ref, halo_ref, filt_ref, rate_ref, out_ref, drive_ref):
    k = _featurize_one(x_ref, halo_ref, filt_ref, 1)
    v = _featurize_one(x_ref, halo_ref, filt_ref, 2)
    drive_ref[...] = k * v
    decay = jnp.exp(-rate_ref[...])
    block = rate_ref.shape[1]
    start = pl.multiple_of(pl.program_id(0) * block, block)
    state = jnp.zeros(rate_ref.shape, jnp.float32)
    out_ref[:, pl.ds(start, block)] = _scan_rows(drive_ref, decay, None, state, None)


def _mix_kernel(x_ref, halo_ref, filt_ref, rate_ref, res_ref, skip_ref, own_ref, partner_ref, other_ref,
                decay_ref, flag_ref, drive_ref, out_ref, fin_ref, conv_scr):
    modes = rate_ref.shape[0]
    first = flag_ref[0:1, 0:1] > 0.5
    in_low = pl.program_id(0) < pl.num_programs(0) // 2
    from_own = jnp.logical_not(jnp.logical_xor(first, in_low))
    halves = jnp.where(from_own, own_ref[...], partner_ref[...])
    entering = halves[:modes]
    fin_ref[...] = halves[modes:]
    init = jnp.where(first, entering, decay_ref[...] * entering + other_ref[...])
    decay = jnp.exp(-rate_ref[...])
    _scan_rows(drive_ref, decay, res_ref[...], init, conv_scr)
    q = _featurize_one(x_ref, halo_ref, filt_ref, 0)
    out_ref[...] = (q * (conv_scr[...] + skip_ref[...] * drive_ref[...])).astype(out_ref.dtype)


def _specs(row_count, modes, taps, features=3, block=CHAN_BLOCK):
    x_spec = pl.BlockSpec((features, row_count, block), lambda j: (0, 0, j))
    halo_spec = pl.BlockSpec((features, taps - 1, block), lambda j: (0, 0, j))
    filt_spec = pl.BlockSpec((features, taps, block), lambda j: (0, 0, j))
    mode_spec = pl.BlockSpec((modes, block), lambda j: (0, j))
    row_spec = pl.BlockSpec((1, block), lambda j: (0, j))
    return x_spec, halo_spec, filt_spec, mode_spec, row_spec


def contributions(projected, halo, short_filters, decay_rate):
    _, row_count, chan_count = projected.shape
    modes = decay_rate.shape[0]
    taps = short_filters.shape[1]
    x_spec, halo_spec, filt_spec, mode_spec, _ = _specs(row_count, modes, taps)
    return pl.pallas_call(
        _contrib_kernel,
        grid=(chan_count // CHAN_BLOCK,),
        in_specs=[x_spec, halo_spec, filt_spec, mode_spec],
        out_specs=[pl.BlockSpec(memory_space=pltpu.VMEM), pl.BlockSpec((row_count, CHAN_BLOCK), lambda j: (0, j))],
        out_shape=[
            jax.ShapeDtypeStruct((modes, chan_count), jnp.float32),
            jax.ShapeDtypeStruct((row_count, chan_count), jnp.float32),
        ],
    )(projected, halo, short_filters, decay_rate)


def mix(projected, halo, short_filters, decay_rate, residue, skip, own, partner, other, shard_decay,
        flag, drive):
    _, row_count, chan_count = projected.shape
    modes = decay_rate.shape[0]
    taps = short_filters.shape[1]
    block = min(CHAN_BLOCK, chan_count // 2)
    x_spec, halo_spec, filt_spec, mode_spec, row_spec = _specs(row_count, modes, taps, 1, block)
    tile_spec = pl.BlockSpec((row_count, block), lambda j: (0, j))
    per_half = chan_count // 2 // block
    half_spec = pl.BlockSpec((2 * modes, block), lambda j: (0, j % per_half))
    flag_spec = pl.BlockSpec(flag.shape, lambda j: (0, 0))
    return pl.pallas_call(
        _mix_kernel,
        grid=(chan_count // block,),
        in_specs=[x_spec, halo_spec, filt_spec, mode_spec, mode_spec, row_spec, half_spec, half_spec,
                  mode_spec, mode_spec, flag_spec, tile_spec],
        out_specs=[tile_spec, mode_spec],
        out_shape=[
            jax.ShapeDtypeStruct((row_count, chan_count), jnp.bfloat16),
            jax.ShapeDtypeStruct((modes, chan_count), jnp.float32),
        ],
        scratch_shapes=[pltpu.VMEM((row_count, block), jnp.float32)],
    )(projected, halo, short_filters, decay_rate, residue, skip[None, :], own, partner, other,
      shard_decay, flag, drive)


def swap_cores(value):
    return lax.ppermute(value, "dec", [(0, 1), (1, 0)])


def local(projected, short_filters, decay_rate, residue, skip):
    tap_count = short_filters.shape[1]
    row_count = projected.shape[1]
    chan_count = projected.shape[2]
    modes = decay_rate.shape[0]
    edge_rows = projected[:, row_count - (tap_count - 1) :, :]
    halo = from_behind(edge_rows, ("ctx", "dec"), 1)
    contribution, drive = contributions(projected, halo, short_filters, decay_rate)
    core = lax.axis_index("dec")
    first = core == 0
    other = swap_cores(contribution)
    shard_decay = jnp.exp(-decay_rate * row_count)
    half = chan_count // 2
    lo = lambda x: x[:, :half]
    hi = lambda x: x[:, half:]
    chip_part = jnp.where(
        first,
        lo(shard_decay) * lo(contribution) + lo(other),
        hi(shard_decay) * hi(other) + hi(contribution),
    )
    half_decay = jnp.where(first, lo(shard_decay), hi(shard_decay))
    received = lax.all_gather(chip_part, "ctx", axis=0, tiled=False)
    chip_here = lax.axis_index("ctx")
    chip_decay = half_decay * half_decay
    running = jnp.zeros_like(chip_part)
    entering = jnp.zeros_like(chip_part)
    for chip in range(received.shape[0]):
        entering = jnp.where(chip_here == chip, running, entering)
        running = chip_decay * running + received[chip]
    both = jnp.concatenate([entering, running], axis=0)
    other_both = swap_cores(both)
    flag = jnp.where(first, jnp.ones((8, 128), jnp.float32), jnp.zeros((8, 128), jnp.float32))
    mixed, final_state = mix(projected, halo, short_filters, decay_rate, residue, skip, both,
                             other_both, other, shard_decay, flag, drive)
    return (mixed, final_state)


def solution(mesh):
    placed = (
        P(None, ("grp", "ctx", "dec"), "chan"),
        P(None, None, "chan"),
        P(None, "chan"),
        P(None, "chan"),
        P("chan"),
    )
    return jax.shard_map(
        local,
        mesh=mesh,
        in_specs=placed,
        out_specs=(P(("grp", "ctx", "dec"), "chan"), P("grp", "chan")),
        check_vma=False,
    )
```

```python
import functools

import jax
import jax.numpy as jnp
from jax import lax
from jax.experimental import pallas as pl
from jax.experimental.pallas import tpu as pltpu
from jax.sharding import PartitionSpec as P

CHAN_BLOCK = 1024
LANE_BLOCK = 512
ROW_GROUP = 8


def from_behind(value, axis, steps):
    count = lax.axis_size(axis)
    initial, last = (max(0, -steps), min(count, count - steps))
    return lax.ppermute(value, axis, [(source, source + steps) for source in range(initial, last)])


def _featurize_one(x_ref, halo_ref, filt_ref, index):
    x = x_ref[index].astype(jnp.float32)
    halo = halo_ref[index].astype(jnp.float32)
    taps = filt_ref[index]
    last = halo[halo.shape[0] - 1 : halo.shape[0]]
    second = halo[halo.shape[0] - 2 : halo.shape[0] - 1]
    body = taps[0:1] * x + taps[1:2] * pltpu.roll(x, 1, 0) + taps[2:3] * pltpu.roll(x, 2, 0)
    head_x = x[:ROW_GROUP]
    rows = lax.broadcasted_iota(jnp.int32, head_x.shape, 0)
    back1 = jnp.where(rows == 0, last, pltpu.roll(head_x, 1, 0))
    back2 = jnp.where(rows == 0, second, jnp.where(rows == 1, last, pltpu.roll(head_x, 2, 0)))
    head = taps[0:1] * head_x + taps[1:2] * back1 + taps[2:3] * back2
    return jnp.concatenate([head, body[ROW_GROUP:]], axis=0)


def _reduce_rows(ys):
    sub = lax.broadcasted_iota(jnp.int32, ys[0].shape, 0)
    low4 = sub < 4
    a = [jnp.where(low4, ys[i], ys[i + 4]) + pltpu.roll(jnp.where(low4, ys[i + 4], ys[i]), 4, 0) for i in range(4)]
    m2 = jnp.bitwise_and(sub, 3) < 2
    b = [jnp.where(m2, a[i] + pltpu.roll(a[i], 6, 0), a[i + 2] + pltpu.roll(a[i + 2], 2, 0)) for i in range(2)]
    m1 = jnp.bitwise_and(sub, 1) == 0
    return jnp.where(m1, b[0] + pltpu.roll(b[0], 7, 0), b[1] + pltpu.roll(b[1], 1, 0))


def _scan_rows(drive_ref, decay, residue, state, conv_ref):
    row_count = drive_ref.shape[0]
    low = slice(0, ROW_GROUP)
    high = slice(ROW_GROUP, 2 * ROW_GROUP)
    finals = []
    for lane_start in range(0, drive_ref.shape[1], LANE_BLOCK):
        lanes = slice(lane_start, lane_start + LANE_BLOCK)
        decay_part = decay[:, lanes]
        residue_part = None if residue is None else residue[:, lanes]

        def body(group, state):
            start = pl.multiple_of(group * ROW_GROUP, ROW_GROUP)
            ys = []
            block = drive_ref[pl.ds(start, ROW_GROUP), lanes]
            for i in range(ROW_GROUP):
                drive_row = jnp.broadcast_to(block[i : i + 1], state.shape)
                state = decay_part * state + drive_row
                if conv_ref is not None:
                    ys.append(residue_part[low] * state[low] + residue_part[high] * state[high])
            if conv_ref is not None:
                conv_ref[pl.ds(start, ROW_GROUP), lanes] = _reduce_rows(ys)
            return state

        finals.append(lax.fori_loop(0, row_count // ROW_GROUP, body, state[:, lanes]))
    return jnp.concatenate(finals, axis=1)


def _contrib_kernel(x_ref, halo_ref, filt_ref, rate_ref, out_ref, drive_ref):
    k = _featurize_one(x_ref, halo_ref, filt_ref, 1)
    v = _featurize_one(x_ref, halo_ref, filt_ref, 2)
    drive_ref[...] = k * v
    decay = jnp.exp(-rate_ref[...])
    block = rate_ref.shape[1]
    start = pl.multiple_of(pl.program_id(0) * block, block)
    state = jnp.zeros(rate_ref.shape, jnp.float32)
    out_ref[:, pl.ds(start, block)] = _scan_rows(drive_ref, decay, None, state, None)


def _mix_kernel(x_ref, halo_ref, filt_ref, rate_ref, res_ref, skip_ref, own_ref, partner_ref, other_ref,
                decay_ref, drive_ref, out_ref, fin_ref, conv_scr):
    modes = rate_ref.shape[0]
    first = lax.axis_index("dec") == 0
    in_low = pl.program_id(0) < pl.num_programs(0) // 2
    from_own = jnp.logical_not(jnp.logical_xor(first, in_low))
    halves = jnp.where(from_own, own_ref[...], partner_ref[...])
    entering = halves[:modes]
    fin_ref[...] = halves[modes:]
    init = jnp.where(first, entering, decay_ref[...] * entering + other_ref[...])
    decay = jnp.exp(-rate_ref[...])
    _scan_rows(drive_ref, decay, res_ref[...], init, conv_scr)
    q = _featurize_one(x_ref, halo_ref, filt_ref, 0)
    out_ref[...] = (q * (conv_scr[...] + skip_ref[...] * drive_ref[...])).astype(out_ref.dtype)


def _specs(row_count, modes, taps, features=3, block=CHAN_BLOCK):
    x_spec = pl.BlockSpec((features, row_count, block), lambda j: (0, 0, j))
    halo_spec = pl.BlockSpec((features, taps - 1, block), lambda j: (0, 0, j))
    filt_spec = pl.BlockSpec((features, taps, block), lambda j: (0, 0, j))
    mode_spec = pl.BlockSpec((modes, block), lambda j: (0, j))
    row_spec = pl.BlockSpec((1, block), lambda j: (0, j))
    return x_spec, halo_spec, filt_spec, mode_spec, row_spec


def contributions(projected, halo, short_filters, decay_rate):
    _, row_count, chan_count = projected.shape
    modes = decay_rate.shape[0]
    taps = short_filters.shape[1]
    x_spec, halo_spec, filt_spec, mode_spec, _ = _specs(row_count, modes, taps)
    return pl.pallas_call(
        _contrib_kernel,
        grid=(chan_count // CHAN_BLOCK,),
        in_specs=[x_spec, halo_spec, filt_spec, mode_spec],
        out_specs=[pl.BlockSpec(memory_space=pltpu.VMEM), pl.BlockSpec((row_count, CHAN_BLOCK), lambda j: (0, j))],
        out_shape=[
            jax.ShapeDtypeStruct((modes, chan_count), jnp.float32),
            jax.ShapeDtypeStruct((row_count, chan_count), jnp.float32),
        ],
    )(projected, halo, short_filters, decay_rate)


def mix(projected, halo, short_filters, decay_rate, residue, skip, own, partner, other, shard_decay,
        drive):
    _, row_count, chan_count = projected.shape
    modes = decay_rate.shape[0]
    taps = short_filters.shape[1]
    block = min(CHAN_BLOCK, chan_count // 2)
    x_spec, halo_spec, filt_spec, mode_spec, row_spec = _specs(row_count, modes, taps, 1, block)
    tile_spec = pl.BlockSpec((row_count, block), lambda j: (0, j))
    per_half = chan_count // 2 // block
    half_spec = pl.BlockSpec((2 * modes, block), lambda j: (0, j % per_half))
    return pl.pallas_call(
        _mix_kernel,
        grid=(chan_count // block,),
        in_specs=[x_spec, halo_spec, filt_spec, mode_spec, mode_spec, row_spec, half_spec, half_spec,
                  mode_spec, mode_spec, tile_spec],
        out_specs=[tile_spec, mode_spec],
        out_shape=[
            jax.ShapeDtypeStruct((row_count, chan_count), jnp.bfloat16),
            jax.ShapeDtypeStruct((modes, chan_count), jnp.float32),
        ],
        scratch_shapes=[pltpu.VMEM((row_count, block), jnp.float32)],
    )(projected, halo, short_filters, decay_rate, residue, skip[None, :], own, partner, other,
      shard_decay, drive)


def swap_cores(value):
    return lax.ppermute(value, "dec", [(0, 1), (1, 0)])


def local(projected, short_filters, decay_rate, residue, skip):
    tap_count = short_filters.shape[1]
    row_count = projected.shape[1]
    chan_count = projected.shape[2]
    modes = decay_rate.shape[0]
    edge_rows = projected[:, row_count - (tap_count - 1) :, :]
    halo = from_behind(edge_rows, ("ctx", "dec"), 1)
    contribution, drive = contributions(projected, halo, short_filters, decay_rate)
    core = lax.axis_index("dec")
    first = core == 0
    other = swap_cores(contribution)
    shard_decay = jnp.exp(-decay_rate * row_count)
    half = chan_count // 2
    lo = lambda x: x[:, :half]
    hi = lambda x: x[:, half:]
    chip_part = jnp.where(
        first,
        lo(shard_decay) * lo(contribution) + lo(other),
        hi(shard_decay) * hi(other) + hi(contribution),
    )
    half_decay = jnp.where(first, lo(shard_decay), hi(shard_decay))
    received = lax.all_gather(chip_part, "ctx", axis=0, tiled=False)
    chip_here = lax.axis_index("ctx")
    chip_decay = half_decay * half_decay
    running = jnp.zeros_like(chip_part)
    entering = jnp.zeros_like(chip_part)
    for chip in range(received.shape[0]):
        entering = jnp.where(chip_here == chip, running, entering)
        running = chip_decay * running + received[chip]
    both = jnp.concatenate([entering, running], axis=0)
    other_both = swap_cores(both)
    mixed, final_state = mix(projected, halo, short_filters, decay_rate, residue, skip, both,
                             other_both, other, shard_decay, drive)
    return (mixed, final_state)


def solution(mesh):
    placed = (
        P(None, ("grp", "ctx", "dec"), "chan"),
        P(None, None, "chan"),
        P(None, "chan"),
        P(None, "chan"),
        P("chan"),
    )
    return jax.shard_map(
        local,
        mesh=mesh,
        in_specs=placed,
        out_specs=(P(("grp", "ctx", "dec"), "chan"), P("grp", "chan")),
        check_vma=False,
    )
```

```python
import functools

import jax
import jax.numpy as jnp
from jax import lax
from jax.experimental import pallas as pl
from jax.experimental.pallas import tpu as pltpu
from jax.sharding import PartitionSpec as P

CHAN_BLOCK = 1024
LANE_BLOCK = 512
ROW_GROUP = 8


def from_behind(value, axis, steps):
    count = lax.axis_size(axis)
    initial, last = (max(0, -steps), min(count, count - steps))
    return lax.ppermute(value, axis, [(source, source + steps) for source in range(initial, last)])


def _featurize_one(x_ref, halo_ref, filt_ref, index):
    x = x_ref[index].astype(jnp.float32)
    halo = halo_ref[index].astype(jnp.float32)
    taps = filt_ref[index]
    last = halo[halo.shape[0] - 1 : halo.shape[0]]
    second = halo[halo.shape[0] - 2 : halo.shape[0] - 1]
    body = taps[0:1] * x + taps[1:2] * pltpu.roll(x, 1, 0) + taps[2:3] * pltpu.roll(x, 2, 0)
    head_x = x[:ROW_GROUP]
    rows = lax.broadcasted_iota(jnp.int32, head_x.shape, 0)
    back1 = jnp.where(rows == 0, last, pltpu.roll(head_x, 1, 0))
    back2 = jnp.where(rows == 0, second, jnp.where(rows == 1, last, pltpu.roll(head_x, 2, 0)))
    head = taps[0:1] * head_x + taps[1:2] * back1 + taps[2:3] * back2
    return jnp.concatenate([head, body[ROW_GROUP:]], axis=0)


def _reduce_rows(ys):
    sub = lax.broadcasted_iota(jnp.int32, ys[0].shape, 0)
    low4 = sub < 4
    a = [jnp.where(low4, ys[i], ys[i + 4]) + pltpu.roll(jnp.where(low4, ys[i + 4], ys[i]), 4, 0) for i in range(4)]
    m2 = jnp.bitwise_and(sub, 3) < 2
    b = [jnp.where(m2, a[i] + pltpu.roll(a[i], 6, 0), a[i + 2] + pltpu.roll(a[i + 2], 2, 0)) for i in range(2)]
    m1 = jnp.bitwise_and(sub, 1) == 0
    return jnp.where(m1, b[0] + pltpu.roll(b[0], 7, 0), b[1] + pltpu.roll(b[1], 1, 0))


def _scan_rows(drive_ref, decay, residue, state, conv_ref):
    row_count = drive_ref.shape[0]
    low = slice(0, ROW_GROUP)
    high = slice(ROW_GROUP, 2 * ROW_GROUP)
    finals = []
    for lane_start in range(0, drive_ref.shape[1], LANE_BLOCK):
        lanes = slice(lane_start, lane_start + LANE_BLOCK)
        decay_part = decay[:, lanes]
        residue_part = None if residue is None else residue[:, lanes]

        def body(group, state):
            start = pl.multiple_of(group * ROW_GROUP, ROW_GROUP)
            ys = []
            block = drive_ref[pl.ds(start, ROW_GROUP), lanes]
            for i in range(ROW_GROUP):
                drive_row = jnp.broadcast_to(block[i : i + 1], state.shape)
                state = decay_part * state + drive_row
                if conv_ref is not None:
                    ys.append(residue_part[low] * state[low] + residue_part[high] * state[high])
            if conv_ref is not None:
                conv_ref[pl.ds(start, ROW_GROUP), lanes] = _reduce_rows(ys)
            return state

        finals.append(lax.fori_loop(0, row_count // ROW_GROUP, body, state[:, lanes]))
    return jnp.concatenate(finals, axis=1)


def _contrib_kernel(x_ref, halo_ref, filt_ref, rate_ref, out_ref, drive_ref):
    k = _featurize_one(x_ref, halo_ref, filt_ref, 1)
    v = _featurize_one(x_ref, halo_ref, filt_ref, 2)
    drive_ref[...] = k * v
    decay = jnp.exp(-rate_ref[...])
    block = rate_ref.shape[1]
    start = pl.multiple_of(pl.program_id(0) * block, block)
    state = jnp.zeros(rate_ref.shape, jnp.float32)
    out_ref[:, pl.ds(start, block)] = _scan_rows(drive_ref, decay, None, state, None)


def _mix_kernel(x_ref, halo_ref, filt_ref, rate_ref, res_ref, skip_ref, init_ref, fin_in_ref, drive_ref,
                out_ref, fin_ref, conv_scr):
    block = rate_ref.shape[1]
    start = pl.multiple_of(pl.program_id(0) * block, block)
    fin_ref[...] = fin_in_ref[:, pl.ds(start, block)]
    decay = jnp.exp(-rate_ref[...])
    _scan_rows(drive_ref, decay, res_ref[...], init_ref[:, pl.ds(start, block)], conv_scr)
    q = _featurize_one(x_ref, halo_ref, filt_ref, 0)
    out_ref[...] = (q * (conv_scr[...] + skip_ref[...] * drive_ref[...])).astype(out_ref.dtype)


def _specs(row_count, modes, taps, features=3):
    x_spec = pl.BlockSpec((features, row_count, CHAN_BLOCK), lambda j: (0, 0, j))
    halo_spec = pl.BlockSpec((features, taps - 1, CHAN_BLOCK), lambda j: (0, 0, j))
    filt_spec = pl.BlockSpec((features, taps, CHAN_BLOCK), lambda j: (0, 0, j))
    mode_spec = pl.BlockSpec((modes, CHAN_BLOCK), lambda j: (0, j))
    row_spec = pl.BlockSpec((1, CHAN_BLOCK), lambda j: (0, j))
    return x_spec, halo_spec, filt_spec, mode_spec, row_spec


def contributions(projected, halo, short_filters, decay_rate):
    _, row_count, chan_count = projected.shape
    modes = decay_rate.shape[0]
    taps = short_filters.shape[1]
    x_spec, halo_spec, filt_spec, mode_spec, _ = _specs(row_count, modes, taps)
    return pl.pallas_call(
        _contrib_kernel,
        grid=(chan_count // CHAN_BLOCK,),
        in_specs=[x_spec, halo_spec, filt_spec, mode_spec],
        out_specs=[pl.BlockSpec(memory_space=pltpu.VMEM), pl.BlockSpec((row_count, CHAN_BLOCK), lambda j: (0, j))],
        out_shape=[
            jax.ShapeDtypeStruct((modes, chan_count), jnp.float32),
            jax.ShapeDtypeStruct((row_count, chan_count), jnp.float32),
        ],
    )(projected, halo, short_filters, decay_rate)


def mix(projected, halo, short_filters, decay_rate, residue, skip, prefix, final_state, drive):
    _, row_count, chan_count = projected.shape
    modes = decay_rate.shape[0]
    taps = short_filters.shape[1]
    x_spec, halo_spec, filt_spec, mode_spec, row_spec = _specs(row_count, modes, taps, 1)
    tile_spec = pl.BlockSpec((row_count, CHAN_BLOCK), lambda j: (0, j))
    whole = pl.BlockSpec(memory_space=pltpu.VMEM)
    return pl.pallas_call(
        _mix_kernel,
        grid=(chan_count // CHAN_BLOCK,),
        in_specs=[x_spec, halo_spec, filt_spec, mode_spec, mode_spec, row_spec, whole, whole, tile_spec],
        out_specs=[tile_spec, mode_spec],
        out_shape=[
            jax.ShapeDtypeStruct((row_count, chan_count), jnp.bfloat16),
            jax.ShapeDtypeStruct((modes, chan_count), jnp.float32),
        ],
        scratch_shapes=[pltpu.VMEM((row_count, CHAN_BLOCK), jnp.float32)],
    )(projected, halo, short_filters, decay_rate, residue, skip[None, :], prefix, final_state, drive)


def gather_chips(part, chip_here):
    chips = lax.axis_size("ctx")
    held = part[None]
    span = 1
    while span < chips:
        pairs = [(i, i ^ span) for i in range(chips)]
        arrived = lax.ppermute(held, "ctx", pairs)
        upper = (chip_here // span) % 2 == 1
        held = jnp.where(
            upper,
            jnp.concatenate([arrived, held], axis=0),
            jnp.concatenate([held, arrived], axis=0),
        )
        span *= 2
    return held


def swap_cores(value):
    return lax.ppermute(value, "dec", [(0, 1), (1, 0)])


def local(projected, short_filters, decay_rate, residue, skip):
    tap_count = short_filters.shape[1]
    row_count = projected.shape[1]
    chan_count = projected.shape[2]
    modes = decay_rate.shape[0]
    edge_rows = projected[:, row_count - (tap_count - 1) :, :]
    halo = from_behind(edge_rows, ("ctx", "dec"), 1)
    contribution, drive = contributions(projected, halo, short_filters, decay_rate)
    core = lax.axis_index("dec")
    first = core == 0
    other = swap_cores(contribution)
    shard_decay = jnp.exp(-decay_rate * row_count)
    half = chan_count // 2
    lo = lambda x: x[:, :half]
    hi = lambda x: x[:, half:]
    chip_part = jnp.where(
        first,
        lo(shard_decay) * lo(contribution) + lo(other),
        hi(shard_decay) * hi(other) + hi(contribution),
    )
    half_decay = jnp.where(first, lo(shard_decay), hi(shard_decay))
    chip_here = lax.axis_index("ctx")
    received = gather_chips(chip_part, chip_here)
    chip_decay = half_decay * half_decay
    running = jnp.zeros_like(chip_part)
    entering = jnp.zeros_like(chip_part)
    for chip in range(received.shape[0]):
        entering = jnp.where(chip_here == chip, running, entering)
        running = chip_decay * running + received[chip]
    both = jnp.concatenate([entering, running], axis=0)
    other_both = swap_cores(both)
    low = jnp.where(first, both, other_both)
    high = jnp.where(first, other_both, both)
    whole = jnp.concatenate([low, high], axis=1)
    chip_entering = whole[:modes]
    final_state = whole[modes:]
    prefix = jnp.where(first, chip_entering, shard_decay * chip_entering + other)
    mixed, final_state = mix(projected, halo, short_filters, decay_rate, residue, skip, prefix,
                             final_state, drive)
    return (mixed, final_state)


def solution(mesh):
    placed = (
        P(None, ("grp", "ctx", "dec"), "chan"),
        P(None, None, "chan"),
        P(None, "chan"),
        P(None, "chan"),
        P("chan"),
    )
    return jax.shard_map(
        local,
        mesh=mesh,
        in_specs=placed,
        out_specs=(P(("grp", "ctx", "dec"), "chan"), P("grp", "chan")),
        check_vma=False,
    )
```

```python
import functools

import jax
import jax.numpy as jnp
from jax import lax
from jax.experimental import pallas as pl
from jax.experimental.pallas import tpu as pltpu
from jax.sharding import PartitionSpec as P

CHAN_BLOCK = 1024
LANE_BLOCK = 512
ROW_GROUP = 8


def from_behind(value, axis, steps):
    count = lax.axis_size(axis)
    initial, last = (max(0, -steps), min(count, count - steps))
    return lax.ppermute(value, axis, [(source, source + steps) for source in range(initial, last)])


def _featurize_one(x_ref, halo_ref, filt_ref, index):
    x = x_ref[index].astype(jnp.float32)
    halo = halo_ref[index].astype(jnp.float32)
    taps = filt_ref[index]
    last = halo[halo.shape[0] - 1 : halo.shape[0]]
    second = halo[halo.shape[0] - 2 : halo.shape[0] - 1]
    body = taps[0:1] * x + taps[1:2] * pltpu.roll(x, 1, 0) + taps[2:3] * pltpu.roll(x, 2, 0)
    head_x = x[:ROW_GROUP]
    rows = lax.broadcasted_iota(jnp.int32, head_x.shape, 0)
    back1 = jnp.where(rows == 0, last, pltpu.roll(head_x, 1, 0))
    back2 = jnp.where(rows == 0, second, jnp.where(rows == 1, last, pltpu.roll(head_x, 2, 0)))
    head = taps[0:1] * head_x + taps[1:2] * back1 + taps[2:3] * back2
    return jnp.concatenate([head, body[ROW_GROUP:]], axis=0)


def _reduce_rows(ys):
    sub = lax.broadcasted_iota(jnp.int32, ys[0].shape, 0)
    low4 = sub < 4
    a = [jnp.where(low4, ys[i], ys[i + 4]) + pltpu.roll(jnp.where(low4, ys[i + 4], ys[i]), 4, 0) for i in range(4)]
    m2 = jnp.bitwise_and(sub, 3) < 2
    b = [jnp.where(m2, a[i] + pltpu.roll(a[i], 6, 0), a[i + 2] + pltpu.roll(a[i + 2], 2, 0)) for i in range(2)]
    m1 = jnp.bitwise_and(sub, 1) == 0
    return jnp.where(m1, b[0] + pltpu.roll(b[0], 7, 0), b[1] + pltpu.roll(b[1], 1, 0))


def _scan_rows(drive_ref, decay, residue, state, conv_ref):
    row_count = drive_ref.shape[0]
    low = slice(0, ROW_GROUP)
    high = slice(ROW_GROUP, 2 * ROW_GROUP)
    finals = []
    for lane_start in range(0, drive_ref.shape[1], LANE_BLOCK):
        lanes = slice(lane_start, lane_start + LANE_BLOCK)
        decay_part = decay[:, lanes]
        residue_part = None if residue is None else residue[:, lanes]

        def body(group, state):
            start = pl.multiple_of(group * ROW_GROUP, ROW_GROUP)
            ys = []
            block = drive_ref[pl.ds(start, ROW_GROUP), lanes]
            for i in range(ROW_GROUP):
                drive_row = jnp.broadcast_to(block[i : i + 1], state.shape)
                state = decay_part * state + drive_row
                if conv_ref is not None:
                    ys.append(residue_part[low] * state[low] + residue_part[high] * state[high])
            if conv_ref is not None:
                conv_ref[pl.ds(start, ROW_GROUP), lanes] = _reduce_rows(ys)
            return state

        finals.append(lax.fori_loop(0, row_count // ROW_GROUP, body, state[:, lanes]))
    return jnp.concatenate(finals, axis=1)


def _contrib_kernel(x_ref, halo_ref, filt_ref, rate_ref, out_ref, drive_ref):
    k = _featurize_one(x_ref, halo_ref, filt_ref, 1)
    v = _featurize_one(x_ref, halo_ref, filt_ref, 2)
    drive_ref[...] = k * v
    decay = jnp.exp(-rate_ref[...])
    block = rate_ref.shape[1]
    start = pl.multiple_of(pl.program_id(0) * block, block)
    state = jnp.zeros(rate_ref.shape, jnp.float32)
    out_ref[:, pl.ds(start, block)] = _scan_rows(drive_ref, decay, None, state, None)


def _mix_kernel(x_ref, halo_ref, filt_ref, rate_ref, res_ref, skip_ref, init_ref, fin_in_ref, drive_ref,
                out_ref, fin_ref, conv_scr):
    block = rate_ref.shape[1]
    start = pl.multiple_of(pl.program_id(0) * block, block)
    fin_ref[...] = fin_in_ref[:, pl.ds(start, block)]
    decay = jnp.exp(-rate_ref[...])
    _scan_rows(drive_ref, decay, res_ref[...], init_ref[:, pl.ds(start, block)], conv_scr)
    q = _featurize_one(x_ref, halo_ref, filt_ref, 0)
    out_ref[...] = (q * (conv_scr[...] + skip_ref[...] * drive_ref[...])).astype(out_ref.dtype)


def _specs(row_count, modes, taps, features=3):
    x_spec = pl.BlockSpec((features, row_count, CHAN_BLOCK), lambda j: (0, 0, j))
    halo_spec = pl.BlockSpec((features, 2 * ROW_GROUP, CHAN_BLOCK), lambda j: (0, 0, j))
    filt_spec = pl.BlockSpec((features, taps, CHAN_BLOCK), lambda j: (0, 0, j))
    mode_spec = pl.BlockSpec((modes, CHAN_BLOCK), lambda j: (0, j))
    row_spec = pl.BlockSpec((1, CHAN_BLOCK), lambda j: (0, j))
    return x_spec, halo_spec, filt_spec, mode_spec, row_spec


def contributions(projected, halo, short_filters, decay_rate):
    _, row_count, chan_count = projected.shape
    modes = decay_rate.shape[0]
    taps = short_filters.shape[1]
    x_spec, halo_spec, filt_spec, mode_spec, _ = _specs(row_count, modes, taps)
    return pl.pallas_call(
        _contrib_kernel,
        grid=(chan_count // CHAN_BLOCK,),
        in_specs=[x_spec, halo_spec, filt_spec, mode_spec],
        out_specs=[pl.BlockSpec(memory_space=pltpu.VMEM), pl.BlockSpec((row_count, CHAN_BLOCK), lambda j: (0, j))],
        out_shape=[
            jax.ShapeDtypeStruct((modes, chan_count), jnp.float32),
            jax.ShapeDtypeStruct((row_count, chan_count), jnp.float32),
        ],
    )(projected, halo, short_filters, decay_rate)


def mix(projected, halo, short_filters, decay_rate, residue, skip, prefix, final_state, drive):
    _, row_count, chan_count = projected.shape
    modes = decay_rate.shape[0]
    taps = short_filters.shape[1]
    x_spec, halo_spec, filt_spec, mode_spec, row_spec = _specs(row_count, modes, taps, 1)
    tile_spec = pl.BlockSpec((row_count, CHAN_BLOCK), lambda j: (0, j))
    whole = pl.BlockSpec(memory_space=pltpu.VMEM)
    return pl.pallas_call(
        _mix_kernel,
        grid=(chan_count // CHAN_BLOCK,),
        in_specs=[x_spec, halo_spec, filt_spec, mode_spec, mode_spec, row_spec, whole, whole, tile_spec],
        out_specs=[tile_spec, mode_spec],
        out_shape=[
            jax.ShapeDtypeStruct((row_count, chan_count), jnp.bfloat16),
            jax.ShapeDtypeStruct((modes, chan_count), jnp.float32),
        ],
        scratch_shapes=[pltpu.VMEM((row_count, CHAN_BLOCK), jnp.float32)],
    )(projected, halo, short_filters, decay_rate, residue, skip[None, :], prefix, final_state, drive)


def swap_cores(value):
    return lax.ppermute(value, "dec", [(0, 1), (1, 0)])


def local(projected, short_filters, decay_rate, residue, skip):
    tap_count = short_filters.shape[1]
    row_count = projected.shape[1]
    chan_count = projected.shape[2]
    modes = decay_rate.shape[0]
    edge_count = min(2 * ROW_GROUP, row_count)
    edge_rows = projected[:, row_count - edge_count :, :]
    halo = from_behind(edge_rows, ("ctx", "dec"), 1)
    contribution, drive = contributions(projected, halo, short_filters, decay_rate)
    core = lax.axis_index("dec")
    first = core == 0
    other = swap_cores(contribution)
    shard_decay = jnp.exp(-decay_rate * row_count)
    half = chan_count // 2
    lo = lambda x: x[:, :half]
    hi = lambda x: x[:, half:]
    chip_part = jnp.where(
        first,
        lo(shard_decay) * lo(contribution) + lo(other),
        hi(shard_decay) * hi(other) + hi(contribution),
    )
    half_decay = jnp.where(first, lo(shard_decay), hi(shard_decay))
    received = lax.all_gather(chip_part, "ctx", axis=0, tiled=False)
    chip_here = lax.axis_index("ctx")
    chip_decay = half_decay * half_decay
    running = jnp.zeros_like(chip_part)
    entering = jnp.zeros_like(chip_part)
    for chip in range(received.shape[0]):
        entering = jnp.where(chip_here == chip, running, entering)
        running = chip_decay * running + received[chip]
    both = jnp.concatenate([entering, running], axis=0)
    other_both = swap_cores(both)
    low = jnp.where(first, both, other_both)
    high = jnp.where(first, other_both, both)
    whole = jnp.concatenate([low, high], axis=1)
    chip_entering = whole[:modes]
    final_state = whole[modes:]
    prefix = jnp.where(first, chip_entering, shard_decay * chip_entering + other)
    mixed, final_state = mix(projected, halo, short_filters, decay_rate, residue, skip, prefix,
                             final_state, drive)
    return (mixed, final_state)


def solution(mesh):
    placed = (
        P(None, ("grp", "ctx", "dec"), "chan"),
        P(None, None, "chan"),
        P(None, "chan"),
        P(None, "chan"),
        P("chan"),
    )
    return jax.shard_map(
        local,
        mesh=mesh,
        in_specs=placed,
        out_specs=(P(("grp", "ctx", "dec"), "chan"), P("grp", "chan")),
        check_vma=False,
    )
```

```python
import functools

import jax
import jax.numpy as jnp
from jax import lax
from jax.experimental import pallas as pl
from jax.experimental.pallas import tpu as pltpu
from jax.sharding import PartitionSpec as P

CHAN_BLOCK = 1024
LANE_BLOCK = 512
ROW_GROUP = 8


def from_behind(value, axis, steps):
    count = lax.axis_size(axis)
    initial, last = (max(0, -steps), min(count, count - steps))
    return lax.ppermute(value, axis, [(source, source + steps) for source in range(initial, last)])


def _featurize_one(x_ref, halo_ref, filt_ref, index):
    x = x_ref[index].astype(jnp.float32)
    halo = halo_ref[index].astype(jnp.float32)
    taps = filt_ref[index]
    last = halo[halo.shape[0] - 1 : halo.shape[0]]
    second = halo[halo.shape[0] - 2 : halo.shape[0] - 1]
    raw = x_ref[index]
    row_count = raw.shape[0]
    to_row = lax.broadcasted_iota(jnp.int32, (row_count, row_count), 0)
    from_row = lax.broadcasted_iota(jnp.int32, (row_count, row_count), 1)
    shift1 = jnp.where(from_row == to_row - 1, 1.0, 0.0).astype(raw.dtype)
    shift2 = jnp.where(from_row == to_row - 2, 1.0, 0.0).astype(raw.dtype)
    moved1 = jnp.dot(shift1, raw, preferred_element_type=jnp.float32)
    moved2 = jnp.dot(shift2, raw, preferred_element_type=jnp.float32)
    body = taps[0:1] * x + taps[1:2] * moved1 + taps[2:3] * moved2
    head_x = x[:ROW_GROUP]
    rows = lax.broadcasted_iota(jnp.int32, head_x.shape, 0)
    back1 = jnp.where(rows == 0, last, pltpu.roll(head_x, 1, 0))
    back2 = jnp.where(rows == 0, second, jnp.where(rows == 1, last, pltpu.roll(head_x, 2, 0)))
    head = taps[0:1] * head_x + taps[1:2] * back1 + taps[2:3] * back2
    return jnp.concatenate([head, body[ROW_GROUP:]], axis=0)


def _reduce_rows(ys):
    sub = lax.broadcasted_iota(jnp.int32, ys[0].shape, 0)
    low4 = sub < 4
    a = [jnp.where(low4, ys[i], ys[i + 4]) + pltpu.roll(jnp.where(low4, ys[i + 4], ys[i]), 4, 0) for i in range(4)]
    m2 = jnp.bitwise_and(sub, 3) < 2
    b = [jnp.where(m2, a[i] + pltpu.roll(a[i], 6, 0), a[i + 2] + pltpu.roll(a[i + 2], 2, 0)) for i in range(2)]
    m1 = jnp.bitwise_and(sub, 1) == 0
    return jnp.where(m1, b[0] + pltpu.roll(b[0], 7, 0), b[1] + pltpu.roll(b[1], 1, 0))


def _scan_rows(drive_ref, decay, residue, state, conv_ref):
    row_count = drive_ref.shape[0]
    low = slice(0, ROW_GROUP)
    high = slice(ROW_GROUP, 2 * ROW_GROUP)
    finals = []
    for lane_start in range(0, drive_ref.shape[1], LANE_BLOCK):
        lanes = slice(lane_start, lane_start + LANE_BLOCK)
        decay_part = decay[:, lanes]
        residue_part = None if residue is None else residue[:, lanes]

        def body(group, state):
            start = pl.multiple_of(group * ROW_GROUP, ROW_GROUP)
            ys = []
            block = drive_ref[pl.ds(start, ROW_GROUP), lanes]
            for i in range(ROW_GROUP):
                drive_row = jnp.broadcast_to(block[i : i + 1], state.shape)
                state = decay_part * state + drive_row
                if conv_ref is not None:
                    ys.append(residue_part[low] * state[low] + residue_part[high] * state[high])
            if conv_ref is not None:
                conv_ref[pl.ds(start, ROW_GROUP), lanes] = _reduce_rows(ys)
            return state

        finals.append(lax.fori_loop(0, row_count // ROW_GROUP, body, state[:, lanes]))
    return jnp.concatenate(finals, axis=1)


def _contrib_kernel(x_ref, halo_ref, filt_ref, rate_ref, out_ref, drive_ref):
    k = _featurize_one(x_ref, halo_ref, filt_ref, 1)
    v = _featurize_one(x_ref, halo_ref, filt_ref, 2)
    drive_ref[...] = k * v
    decay = jnp.exp(-rate_ref[...])
    block = rate_ref.shape[1]
    start = pl.multiple_of(pl.program_id(0) * block, block)
    state = jnp.zeros(rate_ref.shape, jnp.float32)
    out_ref[:, pl.ds(start, block)] = _scan_rows(drive_ref, decay, None, state, None)


def _mix_kernel(x_ref, halo_ref, filt_ref, rate_ref, res_ref, skip_ref, init_ref, fin_in_ref, drive_ref,
                out_ref, fin_ref, conv_scr):
    block = rate_ref.shape[1]
    start = pl.multiple_of(pl.program_id(0) * block, block)
    fin_ref[...] = fin_in_ref[:, pl.ds(start, block)]
    decay = jnp.exp(-rate_ref[...])
    _scan_rows(drive_ref, decay, res_ref[...], init_ref[:, pl.ds(start, block)], conv_scr)
    q = _featurize_one(x_ref, halo_ref, filt_ref, 0)
    out_ref[...] = (q * (conv_scr[...] + skip_ref[...] * drive_ref[...])).astype(out_ref.dtype)


def _specs(row_count, modes, taps, features=3):
    x_spec = pl.BlockSpec((features, row_count, CHAN_BLOCK), lambda j: (0, 0, j))
    halo_spec = pl.BlockSpec((features, taps - 1, CHAN_BLOCK), lambda j: (0, 0, j))
    filt_spec = pl.BlockSpec((features, taps, CHAN_BLOCK), lambda j: (0, 0, j))
    mode_spec = pl.BlockSpec((modes, CHAN_BLOCK), lambda j: (0, j))
    row_spec = pl.BlockSpec((1, CHAN_BLOCK), lambda j: (0, j))
    return x_spec, halo_spec, filt_spec, mode_spec, row_spec


def contributions(projected, halo, short_filters, decay_rate):
    _, row_count, chan_count = projected.shape
    modes = decay_rate.shape[0]
    taps = short_filters.shape[1]
    x_spec, halo_spec, filt_spec, mode_spec, _ = _specs(row_count, modes, taps)
    return pl.pallas_call(
        _contrib_kernel,
        grid=(chan_count // CHAN_BLOCK,),
        in_specs=[x_spec, halo_spec, filt_spec, mode_spec],
        out_specs=[pl.BlockSpec(memory_space=pltpu.VMEM), pl.BlockSpec((row_count, CHAN_BLOCK), lambda j: (0, j))],
        out_shape=[
            jax.ShapeDtypeStruct((modes, chan_count), jnp.float32),
            jax.ShapeDtypeStruct((row_count, chan_count), jnp.float32),
        ],
    )(projected, halo, short_filters, decay_rate)


def mix(projected, halo, short_filters, decay_rate, residue, skip, prefix, final_state, drive):
    _, row_count, chan_count = projected.shape
    modes = decay_rate.shape[0]
    taps = short_filters.shape[1]
    x_spec, halo_spec, filt_spec, mode_spec, row_spec = _specs(row_count, modes, taps, 1)
    tile_spec = pl.BlockSpec((row_count, CHAN_BLOCK), lambda j: (0, j))
    whole = pl.BlockSpec(memory_space=pltpu.VMEM)
    return pl.pallas_call(
        _mix_kernel,
        grid=(chan_count // CHAN_BLOCK,),
        in_specs=[x_spec, halo_spec, filt_spec, mode_spec, mode_spec, row_spec, whole, whole, tile_spec],
        out_specs=[tile_spec, mode_spec],
        out_shape=[
            jax.ShapeDtypeStruct((row_count, chan_count), jnp.bfloat16),
            jax.ShapeDtypeStruct((modes, chan_count), jnp.float32),
        ],
        scratch_shapes=[pltpu.VMEM((row_count, CHAN_BLOCK), jnp.float32)],
    )(projected, halo, short_filters, decay_rate, residue, skip[None, :], prefix, final_state, drive)


def swap_cores(value):
    return lax.ppermute(value, "dec", [(0, 1), (1, 0)])


def local(projected, short_filters, decay_rate, residue, skip):
    tap_count = short_filters.shape[1]
    row_count = projected.shape[1]
    chan_count = projected.shape[2]
    modes = decay_rate.shape[0]
    edge_rows = projected[:, row_count - (tap_count - 1) :, :]
    halo = from_behind(edge_rows, ("ctx", "dec"), 1)
    contribution, drive = contributions(projected, halo, short_filters, decay_rate)
    core = lax.axis_index("dec")
    first = core == 0
    other = swap_cores(contribution)
    shard_decay = jnp.exp(-decay_rate * row_count)
    half = chan_count // 2
    lo = lambda x: x[:, :half]
    hi = lambda x: x[:, half:]
    chip_part = jnp.where(
        first,
        lo(shard_decay) * lo(contribution) + lo(other),
        hi(shard_decay) * hi(other) + hi(contribution),
    )
    half_decay = jnp.where(first, lo(shard_decay), hi(shard_decay))
    received = lax.all_gather(chip_part, "ctx", axis=0, tiled=False)
    chip_here = lax.axis_index("ctx")
    chip_decay = half_decay * half_decay
    running = jnp.zeros_like(chip_part)
    entering = jnp.zeros_like(chip_part)
    for chip in range(received.shape[0]):
        entering = jnp.where(chip_here == chip, running, entering)
        running = chip_decay * running + received[chip]
    both = jnp.concatenate([entering, running], axis=0)
    other_both = swap_cores(both)
    low = jnp.where(first, both, other_both)
    high = jnp.where(first, other_both, both)
    whole = jnp.concatenate([low, high], axis=1)
    chip_entering = whole[:modes]
    final_state = whole[modes:]
    prefix = jnp.where(first, chip_entering, shard_decay * chip_entering + other)
    mixed, final_state = mix(projected, halo, short_filters, decay_rate, residue, skip, prefix,
                             final_state, drive)
    return (mixed, final_state)


def solution(mesh):
    placed = (
        P(None, ("grp", "ctx", "dec"), "chan"),
        P(None, None, "chan"),
        P(None, "chan"),
        P(None, "chan"),
        P("chan"),
    )
    return jax.shard_map(
        local,
        mesh=mesh,
        in_specs=placed,
        out_specs=(P(("grp", "ctx", "dec"), "chan"), P("grp", "chan")),
        check_vma=False,
    )
```

```python
import functools

import jax
import jax.numpy as jnp
from jax import lax
from jax.experimental import pallas as pl
from jax.experimental.pallas import tpu as pltpu
from jax.sharding import PartitionSpec as P

CHAN_BLOCK = 1024
LANE_BLOCK = 512
ROW_GROUP = 8


def from_behind(value, axis, steps):
    count = lax.axis_size(axis)
    initial, last = (max(0, -steps), min(count, count - steps))
    return lax.ppermute(value, axis, [(source, source + steps) for source in range(initial, last)])


def _featurize_one(x_ref, halo_ref, filt_ref, index):
    x = x_ref[index].astype(jnp.float32)
    halo = halo_ref[index].astype(jnp.float32)
    taps = filt_ref[index]
    last = halo[halo.shape[0] - 1 : halo.shape[0]]
    second = halo[halo.shape[0] - 2 : halo.shape[0] - 1]
    body = taps[0:1] * x + taps[1:2] * pltpu.roll(x, 1, 0) + taps[2:3] * pltpu.roll(x, 2, 0)
    head_x = x[:ROW_GROUP]
    rows = lax.broadcasted_iota(jnp.int32, head_x.shape, 0)
    back1 = jnp.where(rows == 0, last, pltpu.roll(head_x, 1, 0))
    back2 = jnp.where(rows == 0, second, jnp.where(rows == 1, last, pltpu.roll(head_x, 2, 0)))
    head = taps[0:1] * head_x + taps[1:2] * back1 + taps[2:3] * back2
    return jnp.concatenate([head, body[ROW_GROUP:]], axis=0)


def _reduce_rows(ys):
    sub = lax.broadcasted_iota(jnp.int32, ys[0].shape, 0)
    low4 = sub < 4
    a = [jnp.where(low4, ys[i], ys[i + 4]) + pltpu.roll(jnp.where(low4, ys[i + 4], ys[i]), 4, 0) for i in range(4)]
    m2 = jnp.bitwise_and(sub, 3) < 2
    b = [jnp.where(m2, a[i] + pltpu.roll(a[i], 6, 0), a[i + 2] + pltpu.roll(a[i + 2], 2, 0)) for i in range(2)]
    m1 = jnp.bitwise_and(sub, 1) == 0
    return jnp.where(m1, b[0] + pltpu.roll(b[0], 7, 0), b[1] + pltpu.roll(b[1], 1, 0))


def _scan_rows(drive_ref, decay, residue, state, conv_ref):
    row_count = drive_ref.shape[0]
    low = slice(0, ROW_GROUP)
    high = slice(ROW_GROUP, 2 * ROW_GROUP)
    finals = []
    for lane_start in range(0, drive_ref.shape[1], LANE_BLOCK):
        lanes = slice(lane_start, lane_start + LANE_BLOCK)
        decay_part = decay[:, lanes]
        residue_part = None if residue is None else residue[:, lanes]

        def body(group, state):
            start = pl.multiple_of(group * ROW_GROUP, ROW_GROUP)
            ys = []
            block = drive_ref[pl.ds(start, ROW_GROUP), lanes]
            for i in range(ROW_GROUP):
                drive_row = jnp.broadcast_to(block[i : i + 1], state.shape)
                state = decay_part * state + drive_row
                if conv_ref is not None:
                    ys.append(residue_part[low] * state[low] + residue_part[high] * state[high])
            if conv_ref is not None:
                conv_ref[pl.ds(start, ROW_GROUP), lanes] = _reduce_rows(ys)
            return state

        finals.append(lax.fori_loop(0, row_count // ROW_GROUP, body, state[:, lanes], unroll=4))
    return jnp.concatenate(finals, axis=1)


def _contrib_kernel(x_ref, halo_ref, filt_ref, rate_ref, out_ref, drive_ref):
    k = _featurize_one(x_ref, halo_ref, filt_ref, 1)
    v = _featurize_one(x_ref, halo_ref, filt_ref, 2)
    drive_ref[...] = k * v
    decay = jnp.exp(-rate_ref[...])
    block = rate_ref.shape[1]
    start = pl.multiple_of(pl.program_id(0) * block, block)
    state = jnp.zeros(rate_ref.shape, jnp.float32)
    out_ref[:, pl.ds(start, block)] = _scan_rows(drive_ref, decay, None, state, None)


def _mix_kernel(x_ref, halo_ref, filt_ref, rate_ref, res_ref, skip_ref, init_ref, fin_in_ref, drive_ref,
                out_ref, fin_ref, conv_scr):
    block = rate_ref.shape[1]
    start = pl.multiple_of(pl.program_id(0) * block, block)
    fin_ref[...] = fin_in_ref[:, pl.ds(start, block)]
    decay = jnp.exp(-rate_ref[...])
    _scan_rows(drive_ref, decay, res_ref[...], init_ref[:, pl.ds(start, block)], conv_scr)
    q = _featurize_one(x_ref, halo_ref, filt_ref, 0)
    out_ref[...] = (q * (conv_scr[...] + skip_ref[...] * drive_ref[...])).astype(out_ref.dtype)


def _specs(row_count, modes, taps, features=3):
    x_spec = pl.BlockSpec((features, row_count, CHAN_BLOCK), lambda j: (0, 0, j))
    halo_spec = pl.BlockSpec((features, taps - 1, CHAN_BLOCK), lambda j: (0, 0, j))
    filt_spec = pl.BlockSpec((features, taps, CHAN_BLOCK), lambda j: (0, 0, j))
    mode_spec = pl.BlockSpec((modes, CHAN_BLOCK), lambda j: (0, j))
    row_spec = pl.BlockSpec((1, CHAN_BLOCK), lambda j: (0, j))
    return x_spec, halo_spec, filt_spec, mode_spec, row_spec


def contributions(projected, halo, short_filters, decay_rate):
    _, row_count, chan_count = projected.shape
    modes = decay_rate.shape[0]
    taps = short_filters.shape[1]
    x_spec, halo_spec, filt_spec, mode_spec, _ = _specs(row_count, modes, taps)
    return pl.pallas_call(
        _contrib_kernel,
        grid=(chan_count // CHAN_BLOCK,),
        in_specs=[x_spec, halo_spec, filt_spec, mode_spec],
        out_specs=[pl.BlockSpec(memory_space=pltpu.VMEM), pl.BlockSpec((row_count, CHAN_BLOCK), lambda j: (0, j))],
        out_shape=[
            jax.ShapeDtypeStruct((modes, chan_count), jnp.float32),
            jax.ShapeDtypeStruct((row_count, chan_count), jnp.float32),
        ],
    )(projected, halo, short_filters, decay_rate)


def mix(projected, halo, short_filters, decay_rate, residue, skip, prefix, final_state, drive):
    _, row_count, chan_count = projected.shape
    modes = decay_rate.shape[0]
    taps = short_filters.shape[1]
    x_spec, halo_spec, filt_spec, mode_spec, row_spec = _specs(row_count, modes, taps, 1)
    tile_spec = pl.BlockSpec((row_count, CHAN_BLOCK), lambda j: (0, j))
    whole = pl.BlockSpec(memory_space=pltpu.VMEM)
    return pl.pallas_call(
        _mix_kernel,
        grid=(chan_count // CHAN_BLOCK,),
        in_specs=[x_spec, halo_spec, filt_spec, mode_spec, mode_spec, row_spec, whole, whole, tile_spec],
        out_specs=[tile_spec, mode_spec],
        out_shape=[
            jax.ShapeDtypeStruct((row_count, chan_count), jnp.bfloat16),
            jax.ShapeDtypeStruct((modes, chan_count), jnp.float32),
        ],
        scratch_shapes=[pltpu.VMEM((row_count, CHAN_BLOCK), jnp.float32)],
    )(projected, halo, short_filters, decay_rate, residue, skip[None, :], prefix, final_state, drive)


def swap_cores(value):
    return lax.ppermute(value, "dec", [(0, 1), (1, 0)])


def local(projected, short_filters, decay_rate, residue, skip):
    tap_count = short_filters.shape[1]
    row_count = projected.shape[1]
    chan_count = projected.shape[2]
    modes = decay_rate.shape[0]
    edge_rows = projected[:, row_count - (tap_count - 1) :, :]
    halo = from_behind(edge_rows, ("ctx", "dec"), 1)
    contribution, drive = contributions(projected, halo, short_filters, decay_rate)
    core = lax.axis_index("dec")
    first = core == 0
    other = swap_cores(contribution)
    shard_decay = jnp.exp(-decay_rate * row_count)
    half = chan_count // 2
    lo = lambda x: x[:, :half]
    hi = lambda x: x[:, half:]
    chip_part = jnp.where(
        first,
        lo(shard_decay) * lo(contribution) + lo(other),
        hi(shard_decay) * hi(other) + hi(contribution),
    )
    half_decay = jnp.where(first, lo(shard_decay), hi(shard_decay))
    received = lax.all_gather(chip_part, "ctx", axis=0, tiled=False)
    chip_here = lax.axis_index("ctx")
    chip_decay = half_decay * half_decay
    running = jnp.zeros_like(chip_part)
    entering = jnp.zeros_like(chip_part)
    for chip in range(received.shape[0]):
        entering = jnp.where(chip_here == chip, running, entering)
        running = chip_decay * running + received[chip]
    both = jnp.concatenate([entering, running], axis=0)
    other_both = swap_cores(both)
    low = jnp.where(first, both, other_both)
    high = jnp.where(first, other_both, both)
    whole = jnp.concatenate([low, high], axis=1)
    chip_entering = whole[:modes]
    final_state = whole[modes:]
    prefix = jnp.where(first, chip_entering, shard_decay * chip_entering + other)
    mixed, final_state = mix(projected, halo, short_filters, decay_rate, residue, skip, prefix,
                             final_state, drive)
    return (mixed, final_state)


def solution(mesh):
    placed = (
        P(None, ("grp", "ctx", "dec"), "chan"),
        P(None, None, "chan"),
        P(None, "chan"),
        P(None, "chan"),
        P("chan"),
    )
    return jax.shard_map(
        local,
        mesh=mesh,
        in_specs=placed,
        out_specs=(P(("grp", "ctx", "dec"), "chan"), P("grp", "chan")),
        check_vma=False,
    )
```

```python
import functools

import jax
import jax.numpy as jnp
from jax import lax
from jax.experimental import pallas as pl
from jax.experimental.pallas import tpu as pltpu
from jax.sharding import PartitionSpec as P

CHAN_BLOCK = 1024
LANE_BLOCK = 512
ROW_GROUP = 8


def from_behind(value, axis, steps):
    count = lax.axis_size(axis)
    initial, last = (max(0, -steps), min(count, count - steps))
    return lax.ppermute(value, axis, [(source, source + steps) for source in range(initial, last)])


def _featurize_one(x_ref, halo_ref, filt_ref, index):
    x = x_ref[index].astype(jnp.float32)
    halo = halo_ref[index].astype(jnp.float32)
    taps = filt_ref[index]
    last = halo[halo.shape[0] - 1 : halo.shape[0]]
    second = halo[halo.shape[0] - 2 : halo.shape[0] - 1]
    body = taps[0:1] * x + taps[1:2] * pltpu.roll(x, 1, 0) + taps[2:3] * pltpu.roll(x, 2, 0)
    head_x = x[:ROW_GROUP]
    rows = lax.broadcasted_iota(jnp.int32, head_x.shape, 0)
    back1 = jnp.where(rows == 0, last, pltpu.roll(head_x, 1, 0))
    back2 = jnp.where(rows == 0, second, jnp.where(rows == 1, last, pltpu.roll(head_x, 2, 0)))
    head = taps[0:1] * head_x + taps[1:2] * back1 + taps[2:3] * back2
    return jnp.concatenate([head, body[ROW_GROUP:]], axis=0)


def _reduce_rows(ys):
    sub = lax.broadcasted_iota(jnp.int32, ys[0].shape, 0)
    low4 = sub < 4
    a = [jnp.where(low4, ys[i], ys[i + 4]) + pltpu.roll(jnp.where(low4, ys[i + 4], ys[i]), 4, 0) for i in range(4)]
    m2 = jnp.bitwise_and(sub, 3) < 2
    b = [jnp.where(m2, a[i] + pltpu.roll(a[i], 6, 0), a[i + 2] + pltpu.roll(a[i + 2], 2, 0)) for i in range(2)]
    m1 = jnp.bitwise_and(sub, 1) == 0
    return jnp.where(m1, b[0] + pltpu.roll(b[0], 7, 0), b[1] + pltpu.roll(b[1], 1, 0))


def _scan_rows(drive_ref, decay, residue, state, conv_ref, unroll=4):
    row_count = drive_ref.shape[0]
    low = slice(0, ROW_GROUP)
    high = slice(ROW_GROUP, 2 * ROW_GROUP)
    finals = []
    for lane_start in range(0, drive_ref.shape[1], LANE_BLOCK):
        lanes = slice(lane_start, lane_start + LANE_BLOCK)
        decay_part = decay[:, lanes]
        residue_part = None if residue is None else residue[:, lanes]

        def body(group, state):
            start = pl.multiple_of(group * ROW_GROUP, ROW_GROUP)
            ys = []
            block = drive_ref[pl.ds(start, ROW_GROUP), lanes]
            for i in range(ROW_GROUP):
                drive_row = jnp.broadcast_to(block[i : i + 1], state.shape)
                state = decay_part * state + drive_row
                if conv_ref is not None:
                    ys.append(residue_part[low] * state[low] + residue_part[high] * state[high])
            if conv_ref is not None:
                conv_ref[pl.ds(start, ROW_GROUP), lanes] = _reduce_rows(ys)
            return state

        finals.append(lax.fori_loop(0, row_count // ROW_GROUP, body, state[:, lanes], unroll=unroll))
    return jnp.concatenate(finals, axis=1)


def _contrib_kernel(x_ref, halo_ref, filt_ref, rate_ref, out_ref, drive_ref):
    k = _featurize_one(x_ref, halo_ref, filt_ref, 1)
    v = _featurize_one(x_ref, halo_ref, filt_ref, 2)
    drive_ref[...] = k * v
    decay = jnp.exp(-rate_ref[...])
    block = rate_ref.shape[1]
    start = pl.multiple_of(pl.program_id(0) * block, block)
    state = jnp.zeros(rate_ref.shape, jnp.float32)
    out_ref[:, pl.ds(start, block)] = _scan_rows(drive_ref, decay, None, state, None, 8)


def _mix_kernel(x_ref, halo_ref, filt_ref, rate_ref, res_ref, skip_ref, init_ref, fin_in_ref, drive_ref,
                out_ref, fin_ref, conv_scr):
    block = rate_ref.shape[1]
    start = pl.multiple_of(pl.program_id(0) * block, block)
    fin_ref[...] = fin_in_ref[:, pl.ds(start, block)]
    decay = jnp.exp(-rate_ref[...])
    _scan_rows(drive_ref, decay, res_ref[...], init_ref[:, pl.ds(start, block)], conv_scr)
    q = _featurize_one(x_ref, halo_ref, filt_ref, 0)
    out_ref[...] = (q * (conv_scr[...] + skip_ref[...] * drive_ref[...])).astype(out_ref.dtype)


def _specs(row_count, modes, taps, features=3):
    x_spec = pl.BlockSpec((features, row_count, CHAN_BLOCK), lambda j: (0, 0, j))
    halo_spec = pl.BlockSpec((features, taps - 1, CHAN_BLOCK), lambda j: (0, 0, j))
    filt_spec = pl.BlockSpec((features, taps, CHAN_BLOCK), lambda j: (0, 0, j))
    mode_spec = pl.BlockSpec((modes, CHAN_BLOCK), lambda j: (0, j))
    row_spec = pl.BlockSpec((1, CHAN_BLOCK), lambda j: (0, j))
    return x_spec, halo_spec, filt_spec, mode_spec, row_spec


def contributions(projected, halo, short_filters, decay_rate):
    _, row_count, chan_count = projected.shape
    modes = decay_rate.shape[0]
    taps = short_filters.shape[1]
    x_spec, halo_spec, filt_spec, mode_spec, _ = _specs(row_count, modes, taps)
    return pl.pallas_call(
        _contrib_kernel,
        grid=(chan_count // CHAN_BLOCK,),
        in_specs=[x_spec, halo_spec, filt_spec, mode_spec],
        out_specs=[pl.BlockSpec(memory_space=pltpu.VMEM), pl.BlockSpec((row_count, CHAN_BLOCK), lambda j: (0, j))],
        out_shape=[
            jax.ShapeDtypeStruct((modes, chan_count), jnp.float32),
            jax.ShapeDtypeStruct((row_count, chan_count), jnp.float32),
        ],
    )(projected, halo, short_filters, decay_rate)


def mix(projected, halo, short_filters, decay_rate, residue, skip, prefix, final_state, drive):
    _, row_count, chan_count = projected.shape
    modes = decay_rate.shape[0]
    taps = short_filters.shape[1]
    x_spec, halo_spec, filt_spec, mode_spec, row_spec = _specs(row_count, modes, taps, 1)
    tile_spec = pl.BlockSpec((row_count, CHAN_BLOCK), lambda j: (0, j))
    whole = pl.BlockSpec(memory_space=pltpu.VMEM)
    return pl.pallas_call(
        _mix_kernel,
        grid=(chan_count // CHAN_BLOCK,),
        in_specs=[x_spec, halo_spec, filt_spec, mode_spec, mode_spec, row_spec, whole, whole, tile_spec],
        out_specs=[tile_spec, mode_spec],
        out_shape=[
            jax.ShapeDtypeStruct((row_count, chan_count), jnp.bfloat16),
            jax.ShapeDtypeStruct((modes, chan_count), jnp.float32),
        ],
        scratch_shapes=[pltpu.VMEM((row_count, CHAN_BLOCK), jnp.float32)],
    )(projected, halo, short_filters, decay_rate, residue, skip[None, :], prefix, final_state, drive)


def swap_cores(value):
    return lax.ppermute(value, "dec", [(0, 1), (1, 0)])


def local(projected, short_filters, decay_rate, residue, skip):
    tap_count = short_filters.shape[1]
    row_count = projected.shape[1]
    chan_count = projected.shape[2]
    modes = decay_rate.shape[0]
    edge_rows = projected[:, row_count - (tap_count - 1) :, :]
    halo = from_behind(edge_rows, ("ctx", "dec"), 1)
    contribution, drive = contributions(projected, halo, short_filters, decay_rate)
    core = lax.axis_index("dec")
    first = core == 0
    other = swap_cores(contribution)
    shard_decay = jnp.exp(-decay_rate * row_count)
    half = chan_count // 2
    lo = lambda x: x[:, :half]
    hi = lambda x: x[:, half:]
    chip_part = jnp.where(
        first,
        lo(shard_decay) * lo(contribution) + lo(other),
        hi(shard_decay) * hi(other) + hi(contribution),
    )
    half_decay = jnp.where(first, lo(shard_decay), hi(shard_decay))
    received = lax.all_gather(chip_part, "ctx", axis=0, tiled=False)
    chip_here = lax.axis_index("ctx")
    chip_decay = half_decay * half_decay
    running = jnp.zeros_like(chip_part)
    entering = jnp.zeros_like(chip_part)
    for chip in range(received.shape[0]):
        entering = jnp.where(chip_here == chip, running, entering)
        running = chip_decay * running + received[chip]
    both = jnp.concatenate([entering, running], axis=0)
    other_both = swap_cores(both)
    low = jnp.where(first, both, other_both)
    high = jnp.where(first, other_both, both)
    whole = jnp.concatenate([low, high], axis=1)
    chip_entering = whole[:modes]
    final_state = whole[modes:]
    prefix = jnp.where(first, chip_entering, shard_decay * chip_entering + other)
    mixed, final_state = mix(projected, halo, short_filters, decay_rate, residue, skip, prefix,
                             final_state, drive)
    return (mixed, final_state)


def solution(mesh):
    placed = (
        P(None, ("grp", "ctx", "dec"), "chan"),
        P(None, None, "chan"),
        P(None, "chan"),
        P(None, "chan"),
        P("chan"),
    )
    return jax.shard_map(
        local,
        mesh=mesh,
        in_specs=placed,
        out_specs=(P(("grp", "ctx", "dec"), "chan"), P("grp", "chan")),
        check_vma=False,
    )
```

```python
import functools

import jax
import jax.numpy as jnp
from jax import lax
from jax.experimental import pallas as pl
from jax.experimental.pallas import tpu as pltpu
from jax.sharding import PartitionSpec as P

CHAN_BLOCK = 1024
LANE_BLOCK = 512
ROW_GROUP = 8


def from_behind(value, axis, steps):
    count = lax.axis_size(axis)
    initial, last = (max(0, -steps), min(count, count - steps))
    return lax.ppermute(value, axis, [(source, source + steps) for source in range(initial, last)])


def _featurize_one(x_ref, halo_ref, filt_ref, index):
    x = x_ref[index].astype(jnp.float32)
    halo = halo_ref[index].astype(jnp.float32)
    taps = filt_ref[index]
    last = halo[halo.shape[0] - 1 : halo.shape[0]]
    second = halo[halo.shape[0] - 2 : halo.shape[0] - 1]
    raw = x_ref[index]
    row_count = raw.shape[0]
    to_row = lax.broadcasted_iota(jnp.int32, (row_count, row_count), 0)
    from_row = lax.broadcasted_iota(jnp.int32, (row_count, row_count), 1)
    shift1 = jnp.where(from_row == to_row - 1, 1.0, 0.0).astype(raw.dtype)
    shift2 = jnp.where(from_row == to_row - 2, 1.0, 0.0).astype(raw.dtype)
    moved1 = jnp.dot(shift1, raw, preferred_element_type=jnp.float32)
    moved2 = jnp.dot(shift2, raw, preferred_element_type=jnp.float32)
    body = taps[0:1] * x + taps[1:2] * moved1 + taps[2:3] * moved2
    head_x = x[:ROW_GROUP]
    rows = lax.broadcasted_iota(jnp.int32, head_x.shape, 0)
    back1 = jnp.where(rows == 0, last, pltpu.roll(head_x, 1, 0))
    back2 = jnp.where(rows == 0, second, jnp.where(rows == 1, last, pltpu.roll(head_x, 2, 0)))
    head = taps[0:1] * head_x + taps[1:2] * back1 + taps[2:3] * back2
    return jnp.concatenate([head, body[ROW_GROUP:]], axis=0)


def _reduce_rows(ys):
    sub = lax.broadcasted_iota(jnp.int32, ys[0].shape, 0)
    low4 = sub < 4
    a = [jnp.where(low4, ys[i], ys[i + 4]) + pltpu.roll(jnp.where(low4, ys[i + 4], ys[i]), 4, 0) for i in range(4)]
    m2 = jnp.bitwise_and(sub, 3) < 2
    b = [jnp.where(m2, a[i] + pltpu.roll(a[i], 6, 0), a[i + 2] + pltpu.roll(a[i + 2], 2, 0)) for i in range(2)]
    m1 = jnp.bitwise_and(sub, 1) == 0
    return jnp.where(m1, b[0] + pltpu.roll(b[0], 7, 0), b[1] + pltpu.roll(b[1], 1, 0))


def _scan_rows(drive_ref, decay, residue, state, conv_ref):
    row_count = drive_ref.shape[0]
    low = slice(0, ROW_GROUP)
    high = slice(ROW_GROUP, 2 * ROW_GROUP)
    finals = []
    for lane_start in range(0, drive_ref.shape[1], LANE_BLOCK):
        lanes = slice(lane_start, lane_start + LANE_BLOCK)
        decay_part = decay[:, lanes]
        residue_part = None if residue is None else residue[:, lanes]

        def body(group, state):
            start = pl.multiple_of(group * ROW_GROUP, ROW_GROUP)
            ys = []
            block = drive_ref[pl.ds(start, ROW_GROUP), lanes]
            for i in range(ROW_GROUP):
                drive_row = jnp.broadcast_to(block[i : i + 1], state.shape)
                state = decay_part * state + drive_row
                if conv_ref is not None:
                    ys.append(residue_part[low] * state[low] + residue_part[high] * state[high])
            if conv_ref is not None:
                conv_ref[pl.ds(start, ROW_GROUP), lanes] = _reduce_rows(ys)
            return state

        finals.append(lax.fori_loop(0, row_count // ROW_GROUP, body, state[:, lanes], unroll=4))
    return jnp.concatenate(finals, axis=1)


def _contrib_kernel(x_ref, halo_ref, filt_ref, rate_ref, out_ref, drive_ref):
    k = _featurize_one(x_ref, halo_ref, filt_ref, 1)
    v = _featurize_one(x_ref, halo_ref, filt_ref, 2)
    drive_ref[...] = k * v
    decay = jnp.exp(-rate_ref[...])
    block = rate_ref.shape[1]
    start = pl.multiple_of(pl.program_id(0) * block, block)
    state = jnp.zeros(rate_ref.shape, jnp.float32)
    out_ref[:, pl.ds(start, block)] = _scan_rows(drive_ref, decay, None, state, None)


def _mix_kernel(x_ref, halo_ref, filt_ref, rate_ref, res_ref, skip_ref, init_ref, fin_in_ref, drive_ref,
                out_ref, fin_ref, conv_scr):
    block = rate_ref.shape[1]
    start = pl.multiple_of(pl.program_id(0) * block, block)
    fin_ref[...] = fin_in_ref[:, pl.ds(start, block)]
    decay = jnp.exp(-rate_ref[...])
    _scan_rows(drive_ref, decay, res_ref[...], init_ref[:, pl.ds(start, block)], conv_scr)
    q = _featurize_one(x_ref, halo_ref, filt_ref, 0)
    out_ref[...] = (q * (conv_scr[...] + skip_ref[...] * drive_ref[...])).astype(out_ref.dtype)


def _specs(row_count, modes, taps, features=3):
    x_spec = pl.BlockSpec((features, row_count, CHAN_BLOCK), lambda j: (0, 0, j))
    halo_spec = pl.BlockSpec((features, taps - 1, CHAN_BLOCK), lambda j: (0, 0, j))
    filt_spec = pl.BlockSpec((features, taps, CHAN_BLOCK), lambda j: (0, 0, j))
    mode_spec = pl.BlockSpec((modes, CHAN_BLOCK), lambda j: (0, j))
    row_spec = pl.BlockSpec((1, CHAN_BLOCK), lambda j: (0, j))
    return x_spec, halo_spec, filt_spec, mode_spec, row_spec


def contributions(projected, halo, short_filters, decay_rate):
    _, row_count, chan_count = projected.shape
    modes = decay_rate.shape[0]
    taps = short_filters.shape[1]
    x_spec, halo_spec, filt_spec, mode_spec, _ = _specs(row_count, modes, taps)
    return pl.pallas_call(
        _contrib_kernel,
        grid=(chan_count // CHAN_BLOCK,),
        in_specs=[x_spec, halo_spec, filt_spec, mode_spec],
        out_specs=[pl.BlockSpec(memory_space=pltpu.VMEM), pl.BlockSpec((row_count, CHAN_BLOCK), lambda j: (0, j))],
        out_shape=[
            jax.ShapeDtypeStruct((modes, chan_count), jnp.float32),
            jax.ShapeDtypeStruct((row_count, chan_count), jnp.float32),
        ],
    )(projected, halo, short_filters, decay_rate)


def mix(projected, halo, short_filters, decay_rate, residue, skip, prefix, final_state, drive):
    _, row_count, chan_count = projected.shape
    modes = decay_rate.shape[0]
    taps = short_filters.shape[1]
    x_spec, halo_spec, filt_spec, mode_spec, row_spec = _specs(row_count, modes, taps, 1)
    tile_spec = pl.BlockSpec((row_count, CHAN_BLOCK), lambda j: (0, j))
    whole = pl.BlockSpec(memory_space=pltpu.VMEM)
    return pl.pallas_call(
        _mix_kernel,
        grid=(chan_count // CHAN_BLOCK,),
        in_specs=[x_spec, halo_spec, filt_spec, mode_spec, mode_spec, row_spec, whole, whole, tile_spec],
        out_specs=[tile_spec, mode_spec],
        out_shape=[
            jax.ShapeDtypeStruct((row_count, chan_count), jnp.bfloat16),
            jax.ShapeDtypeStruct((modes, chan_count), jnp.float32),
        ],
        scratch_shapes=[pltpu.VMEM((row_count, CHAN_BLOCK), jnp.float32)],
    )(projected, halo, short_filters, decay_rate, residue, skip[None, :], prefix, final_state, drive)


def swap_cores(value):
    return lax.ppermute(value, "dec", [(0, 1), (1, 0)])


def local(projected, short_filters, decay_rate, residue, skip):
    tap_count = short_filters.shape[1]
    row_count = projected.shape[1]
    chan_count = projected.shape[2]
    modes = decay_rate.shape[0]
    edge_rows = projected[:, row_count - (tap_count - 1) :, :]
    halo = from_behind(edge_rows, ("ctx", "dec"), 1)
    contribution, drive = contributions(projected, halo, short_filters, decay_rate)
    core = lax.axis_index("dec")
    first = core == 0
    other = swap_cores(contribution)
    shard_decay = jnp.exp(-decay_rate * row_count)
    half = chan_count // 2
    lo = lambda x: x[:, :half]
    hi = lambda x: x[:, half:]
    chip_part = jnp.where(
        first,
        lo(shard_decay) * lo(contribution) + lo(other),
        hi(shard_decay) * hi(other) + hi(contribution),
    )
    half_decay = jnp.where(first, lo(shard_decay), hi(shard_decay))
    received = lax.all_gather(chip_part, "ctx", axis=0, tiled=False)
    chip_here = lax.axis_index("ctx")
    chip_decay = half_decay * half_decay
    running = jnp.zeros_like(chip_part)
    entering = jnp.zeros_like(chip_part)
    for chip in range(received.shape[0]):
        entering = jnp.where(chip_here == chip, running, entering)
        running = chip_decay * running + received[chip]
    both = jnp.concatenate([entering, running], axis=0)
    other_both = swap_cores(both)
    low = jnp.where(first, both, other_both)
    high = jnp.where(first, other_both, both)
    whole = jnp.concatenate([low, high], axis=1)
    chip_entering = whole[:modes]
    final_state = whole[modes:]
    prefix = jnp.where(first, chip_entering, shard_decay * chip_entering + other)
    mixed, final_state = mix(projected, halo, short_filters, decay_rate, residue, skip, prefix,
                             final_state, drive)
    return (mixed, final_state)


def solution(mesh):
    placed = (
        P(None, ("grp", "ctx", "dec"), "chan"),
        P(None, None, "chan"),
        P(None, "chan"),
        P(None, "chan"),
        P("chan"),
    )
    return jax.shard_map(
        local,
        mesh=mesh,
        in_specs=placed,
        out_specs=(P(("grp", "ctx", "dec"), "chan"), P("grp", "chan")),
        check_vma=False,
    )
```
